32 devices in a mesh: grp: 2 (over x), ep: 16 (over z, y, core).
Axes of the slice: x: 2, y: 2, z: 4, core: 2. Of those that a mesh axis runs over, the one named last changes fastest.
Arguments:
- attention: bfloat16 [4096, 1024], P(('grp', 'ep')), may hold values from -6 to 6
- residual: bfloat16 [4096, 1024], P(('grp', 'ep')), may hold values from -6 to 6
- out_proj: bfloat16 [1024, 1024], P(None, 'grp'), may hold values from -0.1875 to 0.1875
- pre_gain: float32 [1024], replicated, may hold values from 0.25 to 1.75
- post_gain: float32 [1024], replicated, may hold values from 0.25 to 1.75
- slot_gate_up: bfloat16 [16, 1024, 1024], P('ep'), may hold values from -0.1875 to 0.1875
- slot_down: bfloat16 [16, 512, 1024], P('ep'), may hold values from -0.25 to 0.25
- expert_ids: int32 [4096, 8], P(('grp', 'ep')), may hold values from 0 to 15, all different within a row
- copy_choice: int32 [4096, 8], P(('grp', 'ep')), may hold values from 0 to 1
- placement: int32 [16], replicated, may hold values from 0 to 15, each once
- request_age: int32 [4096], P(('grp', 'ep')), may hold values from 0 to 1048575
- decode_flag: int32 [4096], P(('grp', 'ep')), may hold values 0 or 1
- capacity: int32 [2, 16], replicated, may hold values from 16 to 32, as said below
- route_weight: float32 [4096, 8], P(('grp', 'ep')), may hold values from 0.05 to 1
Outputs:
- layer_out: bfloat16 [4096, 1024], P(('grp', 'ep'))
The draws below stay inside these ranges and needn't reach their ends.
Inputs may be any that keep to these rules, and one draw needn't show every extreme that they name: At least one block has capacity 32. `expert_ids`: each row names 8 different experts. `placement`: each slot holds a different expert.
All inputs are finite; a program needn't handle non-finite values. No bound on the sum of `decode_flag` on one device may be relied on, other than what follows from the above.
Results may differ from the reference program's by a relative error of at most 0.01.
Values may be sent and summed in bfloat16 or wider, within the bound.
No kernel may reach another device: no remote copies, remote signals or barrier semaphores. Data moves between devices by JAX's collectives and lax.ppermute only.
A program may use at most 64 MiB of HBM per device.

```python
import math
import jax
import jax.numpy as jnp
from jax import lax

D = 1024
FF = 512
TOPK = 8
ROWS_DEV = 128
EXPERTS = 16
ROWS = 4096
CAP = 32
N_GRP = 2
N_EP = 16


def draw_capacity(key, part):
    first, second = jax.random.split(key)
    lowest = max(1, CAP // 2)
    levels = jax.random.randint(first, (N_GRP * N_EP,), lowest, CAP + 1)
    chosen = jax.random.randint(second, (), 0, N_GRP * N_EP)
    levels = levels.at[chosen].set(CAP)
    return levels.reshape(N_GRP, N_EP).astype(jnp.int32)


def draw_request_age(key, part):
    first, second = jax.random.split(jax.random.fold_in(key, 17))
    ages = jax.random.randint(first, (ROWS,), 0, 64)
    chosen = jax.random.randint(second, (), 0, ROWS)
    ages = ages.at[chosen].set(1048575)
    ages = ages.at[(chosen + 1) % ROWS].set(0)
    return ages.astype(jnp.int32)


def with_ends(values, own_key, smallest, largest):
    spot = [jax.random.randint(jax.random.fold_in(own_key, axis), (), 0, length) for axis, length in enumerate(values.shape)]
    main_axis = values.shape.index(max(values.shape))
    neighbour = spot[:main_axis] + [(spot[main_axis] + 1) % values.shape[main_axis]] + spot[main_axis + 1:]
    return values.at[tuple(spot)].set(smallest).at[tuple(neighbour)].set(largest)


def block_levels(rng, extent, shards, smallest, largest):
    def one(dim, shards_of):
        steps = jax.random.uniform(jax.random.fold_in(jax.random.fold_in(rng, 6), dim), (shards_of,), jnp.float32, smallest / len(shards), largest / len(shards))
        return jnp.repeat(jnp.exp(steps), extent[dim] // shards_of).reshape((-1,) + (1,) * (len(extent) - dim - 1))

    loudness = one(*shards[0])
    for cut in shards[1:]:
        loudness = loudness * one(*cut)
    return loudness


def distinct(rng, rows, amount, top, lift):
    ranking = jax.random.permutation(jax.random.fold_in(rng, 1), amount)
    favour = ranking
    for power in range(3):
        favour = favour * favour // amount
    favour = favour * lift // amount
    chance = jax.random.randint(jax.random.fold_in(rng, 2), (rows, amount), 0, 4096) + favour
    fixed_rows = jax.random.permutation(jax.random.fold_in(rng, 3), rows)[jnp.arange(amount) % rows]
    chance = jnp.where(jnp.arange(rows)[:, None] == fixed_rows[None, :], 1 << 14, chance)
    score = chance * amount + jnp.arange(amount)
    return lax.top_k(score.astype(jnp.int32), top)[1].astype(jnp.int32)


def gaussian(stream_key, shape, width, reach, cuts=(), kind=jnp.bfloat16):
    entries = width * jax.random.normal(stream_key, shape, jnp.float32)
    if cuts:
        entries = entries * block_levels(stream_key, shape, cuts, -0.22, 0.18)
    return jnp.clip(entries, -reach, reach).astype(kind)


def setup_inputs(seed: int = 0) -> dict:
    keys = jax.random.split(jax.random.key(seed), 15)
    return {
        "attention": gaussian(keys[0], (ROWS, D), 1.0, 6.0, ((0, 32),)),
        "residual": gaussian(keys[1], (ROWS, D), 1.0, 6.0, ((0, 32),)),
        "out_proj": gaussian(keys[2], (D, D), D ** -0.5, 0.1875, ((1, 2),)),
        "pre_gain": jnp.clip(1.0 + 0.15 * jax.random.normal(keys[3], (D,), jnp.float32), 0.25, 1.75),
        "post_gain": jnp.clip(1.0 + 0.15 * jax.random.normal(keys[4], (D,), jnp.float32), 0.25, 1.75),
        "slot_gate_up": gaussian(keys[5], (N_EP, D, 2 * FF), D ** -0.5, 0.1875, ((0, 16),)),
        "slot_down": gaussian(keys[6], (N_EP, FF, D), FF ** -0.5, 0.25, ((0, 16),)),
        "expert_ids": distinct(keys[7], ROWS, EXPERTS, TOPK, 8192),
        "copy_choice": with_ends(jax.random.randint(keys[8], (ROWS, TOPK), 0, N_GRP), jax.random.fold_in(keys[8], 1), 0, N_GRP - 1).astype(jnp.int32),
        "placement": jax.random.permutation(keys[9], N_EP).astype(jnp.int32),
        "request_age": draw_request_age(jax.random.fold_in(keys[14], 71), 0),
        "decode_flag": with_ends((jax.random.randint(keys[11], (ROWS,), 0, 3) < 1).astype(jnp.int32), jax.random.fold_in(keys[11], 1), 0, 1),
        "capacity": draw_capacity(jax.random.fold_in(keys[14], 71), 0),
        "route_weight": jnp.clip(jnp.exp(math.log(1.0) - 2.9957323 * jax.random.uniform(keys[13], (ROWS, TOPK), jnp.float32) ** block_levels(keys[13], (ROWS, TOPK), ((0, 32),), -0.2, 0.2)), 0.05, 1.0),
    }


def rms_scale(values, gain):
    meansq = lax.optimization_barrier(jnp.mean(values * values, axis=-1, keepdims=True))
    return values * lax.rsqrt(meansq + 1e-06) * gain

def reference(attention, residual, out_proj, pre_gain, post_gain, slot_gate_up, slot_down, expert_ids, copy_choice, placement, request_age, decode_flag, capacity, route_weight):
    devices_all = N_GRP * N_EP
    attn_proj = jnp.dot(attention, out_proj, preferred_element_type=jnp.float32)
    hidden_state = (residual.astype(jnp.float32) + attn_proj).astype(jnp.bfloat16)
    normed = rms_scale(hidden_state.astype(jnp.float32), pre_gain).astype(jnp.bfloat16)
    slot_table = jnp.arange(N_EP, dtype=jnp.int32)
    matches = (placement[None, :] == jnp.arange(EXPERTS, dtype=jnp.int32)[:, None]).astype(jnp.int32)
    slot_of = lax.optimization_barrier(jnp.sum(slot_table[None, :] * matches, axis=1)).astype(jnp.int32)
    target = (copy_choice * N_EP + slot_of[expert_ids]).astype(jnp.int32)
    priority = (decode_flag * 1048576 + request_age).astype(jnp.int32)

    def block_position(pieces):
        target_block, priority_block = pieces
        hits = lax.optimization_barrier(jnp.sum((target_block[:, :, None] == jnp.arange(devices_all, dtype=jnp.int32)[None, None, :]).astype(jnp.float32), axis=1))
        order = jnp.arange(ROWS_DEV, dtype=jnp.int32)
        ahead_mask = (priority_block[None, :] > priority_block[:, None]) | (priority_block[None, :] == priority_block[:, None]) & (order[None, :] < order[:, None])
        counts = jnp.dot(ahead_mask.astype(jnp.float32), hits, precision=lax.Precision.HIGHEST)
        return jnp.take_along_axis(counts, target_block, axis=1).astype(jnp.int32)
    position = lax.map(block_position, (target.reshape(devices_all, ROWS_DEV, TOPK), priority.reshape(devices_all, ROWS_DEV)))
    position = position.reshape(ROWS, TOPK)
    accepted = position < capacity.reshape(-1)[target]
    source = (jnp.arange(ROWS, dtype=jnp.int32) // ROWS_DEV)[:, None]
    total_slots = devices_all * devices_all * CAP
    index = jnp.where(accepted, target * (devices_all * CAP) + source * CAP + position, total_slots).astype(jnp.int32)
    spread_rows = jnp.broadcast_to(normed[:, None, :], (ROWS, TOPK, D)).reshape(ROWS * TOPK, D)
    buffer = jnp.zeros((total_slots, D), jnp.bfloat16).at[index.reshape(-1)].set(spread_rows, mode='drop')

    def apply_expert(pieces):
        slot_rows, slot = pieces
        gate_up = jnp.dot(slot_rows, slot_gate_up[slot], preferred_element_type=jnp.float32)
        expert_hidden = (jax.nn.silu(gate_up[:, :FF]) * gate_up[:, FF:]).astype(jnp.bfloat16)
        return jnp.dot(expert_hidden, slot_down[slot], preferred_element_type=jnp.float32).astype(jnp.bfloat16)
    slots = jnp.arange(devices_all, dtype=jnp.int32) % N_EP
    results = lax.map(apply_expert, (buffer.reshape(devices_all, devices_all * CAP, D), slots)).reshape(total_slots, D)
    expert_out = results[jnp.minimum(index, total_slots - 1)]
    weights_kept = jnp.where(accepted, route_weight, jnp.float32(0.0))
    mixture = jnp.einsum('rk,rkd->rd', weights_kept, expert_out.astype(jnp.float32))
    return rms_scale(hidden_state.astype(jnp.float32) + mixture, post_gain).astype(jnp.bfloat16)
```

```python
import jax
import jax.numpy as jnp
from jax import lax
from jax.sharding import PartitionSpec as P


def rms_scale(values, gain):
    meansq = jnp.mean(values * values, axis=-1, keepdims=True)
    return values * lax.rsqrt(meansq + 1e-06) * gain


def on_device(
    attention,
    residual,
    out_proj,
    pre_gain,
    post_gain,
    slot_gate_up,
    slot_down,
    expert_ids,
    copy_choice,
    placement,
    request_age,
    decode_flag,
    capacity,
    route_weight,
):
    groups = lax.axis_size("grp")
    owners = lax.axis_size("ep")
    devices_all = groups * owners
    rows_here = attention.shape[0]
    features = attention.shape[1]
    picks_row = expert_ids.shape[1]
    cap_size = max(2, rows_here * picks_row // devices_all)
    columns = jnp.dot(
        lax.all_gather(attention, "grp", axis=0, tiled=True),
        out_proj,
        preferred_element_type=jnp.float32,
    )
    attn_proj = lax.all_to_all(columns, "grp", split_axis=0, concat_axis=1, tiled=True)
    hidden_state = (residual.astype(jnp.float32) + attn_proj).astype(jnp.bfloat16)
    normed = rms_scale(hidden_state.astype(jnp.float32), pre_gain).astype(jnp.bfloat16)
    experts_all = placement.shape[0]
    slot_table = jnp.arange(owners, dtype=jnp.int32)
    matches = (placement[None, :] == jnp.arange(experts_all, dtype=jnp.int32)[:, None]).astype(
        jnp.int32
    )
    slot_of = jnp.sum(slot_table[None, :] * matches, axis=1)
    expert_hits = (
        expert_ids[:, :, None] == jnp.arange(experts_all, dtype=jnp.int32)[None, None, :]
    ).astype(jnp.int32)
    target = copy_choice * owners + jnp.sum(expert_hits * slot_of[None, None, :], axis=2)
    priority = decode_flag * 1048576 + request_age
    order = jnp.arange(rows_here, dtype=jnp.int32)
    ahead_mask = (priority[None, :] > priority[:, None]) | (
        priority[None, :] == priority[:, None]
    ) & (order[None, :] < order[:, None])
    target_onehot = target[:, :, None] == jnp.arange(devices_all, dtype=jnp.int32)[None, None, :]
    target_hits = jnp.sum(target_onehot.astype(jnp.bfloat16), axis=1)
    counts = jnp.dot(
        ahead_mask.astype(jnp.bfloat16), target_hits, preferred_element_type=jnp.float32
    )
    position = jnp.sum(
        jnp.where(target_onehot, counts[:, None, :], 0.0), axis=2
    ).astype(jnp.int32)
    granted = jnp.sum(
        jnp.where(target_onehot, capacity.reshape(-1)[None, None, :], 0), axis=2
    )
    accepted = position < granted
    total_slots = devices_all * cap_size
    index = jnp.where(accepted, target * cap_size + position, total_slots)
    slot_ids = jnp.arange(total_slots, dtype=jnp.int32)
    dispatch = jnp.any(index[None, :, :] == slot_ids[:, None, None], axis=2).astype(jnp.bfloat16)
    buffer = jnp.dot(dispatch, normed, preferred_element_type=jnp.float32).astype(jnp.bfloat16)
    gate_up_local = slot_gate_up[0]
    down_local = slot_down[0]
    hidden_units = down_local.shape[0]
    arrived = lax.all_to_all(
        buffer.reshape(devices_all, cap_size, features),
        ("grp", "ep"),
        split_axis=0,
        concat_axis=0,
        tiled=True,
    )
    flattened = arrived.reshape(-1, features)
    gate_up = jnp.dot(flattened, gate_up_local, preferred_element_type=jnp.float32)
    expert_hidden = (jax.nn.silu(gate_up[:, :hidden_units]) * gate_up[:, hidden_units:]).astype(
        jnp.bfloat16
    )
    produced = jnp.dot(expert_hidden, down_local, preferred_element_type=jnp.float32).astype(
        jnp.bfloat16
    )
    returned = lax.all_to_all(
        produced.reshape(arrived.shape), ("grp", "ep"), split_axis=0, concat_axis=0, tiled=True
    )
    flat_back = returned.reshape(total_slots, features)
    weights_kept = jnp.where(accepted, route_weight, jnp.float32(0.0))
    combine = jnp.sum(
        jnp.where(index[:, :, None] == slot_ids[None, None, :], weights_kept[:, :, None], 0.0),
        axis=1,
    )
    mixture = jnp.dot(
        combine,
        flat_back.astype(jnp.float32),
        precision=lax.Precision.HIGHEST,
        preferred_element_type=jnp.float32,
    )
    return rms_scale(hidden_state.astype(jnp.float32) + mixture, post_gain).astype(jnp.bfloat16)


def solution(mesh):
    placed = (
        P(("grp", "ep"), None),
        P(("grp", "ep"), None),
        P(None, "grp"),
        P(),
        P(),
        P("ep", None, None),
        P("ep", None, None),
        P(("grp", "ep"), None),
        P(("grp", "ep"), None),
        P(),
        P(("grp", "ep")),
        P(("grp", "ep")),
        P(),
        P(("grp", "ep"), None),
    )
    return jax.shard_map(
        on_device, mesh=mesh, in_specs=placed, out_specs=P(("grp", "ep"), None), check_vma=False
    )
```

```python
import jax
import jax.numpy as jnp
import numpy as np
from jax import lax
from jax.sharding import Mesh
from jax.sharding import PartitionSpec as P

ROWS_AXES = ("grp", "eh", "el")
SLOT_AXES = ("eh", "el")
PLANE_AXES = ("grp", "el")


def rms_scale(values, gain):
    meansq = jnp.mean(values * values, axis=-1, keepdims=True)
    return values * lax.rsqrt(meansq + 1e-06) * gain


def on_device(
    attention,
    residual,
    out_proj,
    pre_gain,
    post_gain,
    slot_gate_up,
    slot_down,
    expert_ids,
    copy_choice,
    placement,
    request_age,
    decode_flag,
    capacity,
    route_weight,
):
    groups = lax.axis_size("grp")
    planes = lax.axis_size("eh")
    lanes = lax.axis_size("el")
    owners = planes * lanes
    devices_all = groups * owners
    rows_here = attention.shape[0]
    features = attention.shape[1]
    picks_row = expert_ids.shape[1]
    cap_size = max(2, rows_here * picks_row // devices_all)
    plane_slots = groups * lanes * cap_size
    my_plane = lax.axis_index("eh")

    columns = jnp.dot(
        lax.all_gather(attention, "grp", axis=0, tiled=True),
        out_proj,
        preferred_element_type=jnp.float32,
    )
    attn_proj = lax.all_to_all(columns, "grp", split_axis=0, concat_axis=1, tiled=True)
    hidden_state = (residual.astype(jnp.float32) + attn_proj).astype(jnp.bfloat16)
    normed = rms_scale(hidden_state.astype(jnp.float32), pre_gain).astype(jnp.bfloat16)

    experts_all = placement.shape[0]
    slot_table = jnp.arange(owners, dtype=jnp.int32)
    matches = (placement[None, :] == jnp.arange(experts_all, dtype=jnp.int32)[:, None]).astype(
        jnp.int32
    )
    slot_of = jnp.sum(slot_table[None, :] * matches, axis=1)
    expert_hits = (
        expert_ids[:, :, None] == jnp.arange(experts_all, dtype=jnp.int32)[None, None, :]
    ).astype(jnp.int32)
    slot = jnp.sum(expert_hits * slot_of[None, None, :], axis=2)
    target = copy_choice * owners + slot
    priority = decode_flag * 1048576 + request_age
    order = jnp.arange(rows_here, dtype=jnp.int32)
    ahead_mask = (priority[None, :] > priority[:, None]) | (
        priority[None, :] == priority[:, None]
    ) & (order[None, :] < order[:, None])
    target_onehot = target[:, :, None] == jnp.arange(devices_all, dtype=jnp.int32)[None, None, :]
    target_hits = jnp.sum(target_onehot.astype(jnp.bfloat16), axis=1)
    counts = jnp.dot(
        ahead_mask.astype(jnp.bfloat16), target_hits, preferred_element_type=jnp.float32
    )
    position = jnp.sum(
        jnp.where(target_onehot, counts[:, None, :], 0.0), axis=2
    ).astype(jnp.int32)
    granted = jnp.sum(
        jnp.where(target_onehot, capacity.reshape(-1)[None, None, :], 0), axis=2
    )
    accepted = position < granted
    in_plane = (copy_choice * lanes + slot % lanes) * cap_size + position
    code = jnp.where(accepted, (slot // lanes) * plane_slots + in_plane, planes * plane_slots)
    weights_kept = jnp.where(accepted, route_weight, jnp.float32(0.0))
    meta = jnp.concatenate([code.astype(jnp.float32), weights_kept], axis=1)

    meta_all = lax.all_gather(meta, "eh", axis=0)
    normed_all = lax.all_gather(normed, "eh", axis=0)
    local = meta_all[:, :, :picks_row].astype(jnp.int32) - my_plane * plane_slots
    weights_all = meta_all[:, :, picks_row:]
    slot_ids = jnp.arange(plane_slots, dtype=jnp.int32)
    hit = local[:, None, :, :] == slot_ids[None, :, None, None]
    dispatch = jnp.any(hit, axis=3).astype(jnp.bfloat16)
    buffer = jnp.einsum(
        "hcr,hrd->hcd", dispatch, normed_all, preferred_element_type=jnp.float32
    ).astype(jnp.bfloat16)

    gate_up_local = slot_gate_up[0]
    down_local = slot_down[0]
    hidden_units = down_local.shape[0]
    arrived = lax.all_to_all(
        buffer.reshape(planes, groups * lanes, cap_size, features),
        PLANE_AXES,
        split_axis=1,
        concat_axis=1,
        tiled=True,
    )
    flattened = arrived.reshape(-1, features)
    gate_up = jnp.dot(flattened, gate_up_local, preferred_element_type=jnp.float32)
    expert_hidden = (jax.nn.silu(gate_up[:, :hidden_units]) * gate_up[:, hidden_units:]).astype(
        jnp.bfloat16
    )
    produced = jnp.dot(expert_hidden, down_local, preferred_element_type=jnp.float32).astype(
        jnp.bfloat16
    )
    returned = lax.all_to_all(
        produced.reshape(arrived.shape), PLANE_AXES, split_axis=1, concat_axis=1, tiled=True
    )
    combine = jnp.sum(jnp.where(hit, weights_all[:, None, :, :], 0.0), axis=3)
    partial = jnp.einsum(
        "hcr,hcd->hrd",
        combine,
        returned.reshape(planes, plane_slots, features).astype(jnp.float32),
        precision=lax.Precision.HIGHEST,
        preferred_element_type=jnp.float32,
    )
    mixture = lax.psum_scatter(partial, "eh", scatter_dimension=0, tiled=True)[0]
    return rms_scale(hidden_state.astype(jnp.float32) + mixture, post_gain).astype(jnp.bfloat16)


def plane_split(devices):
    row = devices[0]
    try:
        coords = [tuple(d.coords) for d in row]
    except AttributeError:
        return 1, len(row)
    best = 0
    for axis in range(len(coords[0])):
        changes = [e for e in range(len(row)) if coords[e][axis] != coords[0][axis]]
        if changes:
            best = max(best, changes[0])
    if best == 0 or len(row) % best:
        return 1, len(row)
    return len(row) // best, best


def solution(mesh):
    devices = np.asarray(mesh.devices)
    planes, lanes = plane_split(devices)
    fine = Mesh(devices.reshape(devices.shape[0], planes, lanes), ROWS_AXES)
    rows = P(ROWS_AXES, None)
    placed = (
        rows,
        rows,
        P(None, "grp"),
        P(),
        P(),
        P(SLOT_AXES, None, None),
        P(SLOT_AXES, None, None),
        rows,
        rows,
        P(),
        P(ROWS_AXES),
        P(ROWS_AXES),
        P(),
        rows,
    )
    return jax.shard_map(on_device, mesh=fine, in_specs=placed, out_specs=rows, check_vma=False)
```

```python
import jax
import jax.numpy as jnp
import numpy as np
from jax import lax
from jax.sharding import Mesh
from jax.sharding import PartitionSpec as P

ROWS_AXES = ("grp", "eh", "el")
SLOT_AXES = ("eh", "el")
PLANE_AXES = ("grp", "el")


def rms_scale(values, gain):
    meansq = jnp.mean(values * values, axis=-1, keepdims=True)
    return values * lax.rsqrt(meansq + 1e-06) * gain


def on_device(
    attention,
    residual,
    out_proj,
    pre_gain,
    post_gain,
    slot_gate_up,
    slot_down,
    expert_ids,
    copy_choice,
    placement,
    request_age,
    decode_flag,
    capacity,
    route_weight,
):
    groups = lax.axis_size("grp")
    planes = lax.axis_size("eh")
    lanes = lax.axis_size("el")
    owners = planes * lanes
    devices_all = groups * owners
    rows_here = attention.shape[0]
    features = attention.shape[1]
    picks_row = expert_ids.shape[1]
    cap_size = max(2, rows_here * picks_row // devices_all)
    plane_slots = groups * lanes * cap_size
    my_plane = lax.axis_index("eh")

    columns = jnp.dot(
        lax.all_gather(attention, "grp", axis=0, tiled=True),
        out_proj,
        preferred_element_type=jnp.float32,
    )
    attn_proj = lax.all_to_all(columns, "grp", split_axis=0, concat_axis=1, tiled=True)
    hidden_state = (residual.astype(jnp.float32) + attn_proj).astype(jnp.bfloat16)
    normed = rms_scale(hidden_state.astype(jnp.float32), pre_gain).astype(jnp.bfloat16)

    experts_all = placement.shape[0]
    slot_table = jnp.arange(owners, dtype=jnp.int32)
    matches = (placement[None, :] == jnp.arange(experts_all, dtype=jnp.int32)[:, None]).astype(
        jnp.int32
    )
    slot_of = jnp.sum(slot_table[None, :] * matches, axis=1)
    expert_hits = (
        expert_ids[:, :, None] == jnp.arange(experts_all, dtype=jnp.int32)[None, None, :]
    ).astype(jnp.int32)
    slot = jnp.sum(expert_hits * slot_of[None, None, :], axis=2)
    target = copy_choice * owners + slot
    priority = decode_flag * 1048576 + request_age
    order = jnp.arange(rows_here, dtype=jnp.int32)
    ahead_mask = (priority[None, :] > priority[:, None]) | (
        priority[None, :] == priority[:, None]
    ) & (order[None, :] < order[:, None])
    target_onehot = target[:, :, None] == jnp.arange(devices_all, dtype=jnp.int32)[None, None, :]
    target_hits = jnp.sum(target_onehot.astype(jnp.bfloat16), axis=1)
    counts = jnp.dot(
        ahead_mask.astype(jnp.bfloat16), target_hits, preferred_element_type=jnp.float32
    )
    position = jnp.sum(
        jnp.where(target_onehot, counts[:, None, :], 0.0), axis=2
    ).astype(jnp.int32)
    granted = jnp.sum(
        jnp.where(target_onehot, capacity.reshape(-1)[None, None, :], 0), axis=2
    )
    accepted = position < granted
    in_plane = (copy_choice * lanes + slot % lanes) * cap_size + position
    code = jnp.where(accepted, (slot // lanes) * plane_slots + in_plane, planes * plane_slots)
    weights_kept = jnp.where(accepted, route_weight, jnp.float32(0.0))
    code_hi = (code // 128).astype(jnp.bfloat16)
    code_lo = (code % 128).astype(jnp.bfloat16)
    w_first = lax.reduce_precision(weights_kept, exponent_bits=8, mantissa_bits=7)
    w_rest = weights_kept - w_first
    w_second = lax.reduce_precision(w_rest, exponent_bits=8, mantissa_bits=7)
    w_third = w_rest - w_second
    meta = jnp.concatenate(
        [code_hi, code_lo]
        + [part.astype(jnp.bfloat16) for part in (w_first, w_second, w_third)],
        axis=1,
    )
    meta_size = rows_here * meta.shape[1]
    meta_rows = -(-meta_size // (8 * features)) * 8
    meta_block = jnp.pad(meta.reshape(-1), (0, meta_rows * features - meta_size))
    packed = jnp.concatenate([normed, meta_block.reshape(meta_rows, features)], axis=0)
    packed_all = lax.all_gather(packed, "eh", axis=0)
    normed_all = packed_all[:, :rows_here]
    meta_all = (
        packed_all[:, rows_here:]
        .reshape(planes, -1)[:, :meta_size]
        .reshape(planes, rows_here, meta.shape[1])
        .astype(jnp.float32)
    )
    code_all = meta_all[:, :, :picks_row] * 128 + meta_all[:, :, picks_row : 2 * picks_row]
    local = code_all.astype(jnp.int32) - my_plane * plane_slots
    weights_all = (
        meta_all[:, :, 2 * picks_row : 3 * picks_row]
        + meta_all[:, :, 3 * picks_row : 4 * picks_row]
    ) + meta_all[:, :, 4 * picks_row :]
    slot_ids = jnp.arange(plane_slots, dtype=jnp.int32)
    hit = local[:, None, :, :] == slot_ids[None, :, None, None]
    dispatch = jnp.any(hit, axis=3).astype(jnp.bfloat16)
    buffer = jnp.einsum(
        "hcr,hrd->hcd", dispatch, normed_all, preferred_element_type=jnp.float32
    ).astype(jnp.bfloat16)

    gate_up_local = slot_gate_up[0]
    down_local = slot_down[0]
    hidden_units = down_local.shape[0]
    arrived = lax.all_to_all(
        buffer.reshape(planes, groups * lanes, cap_size, features),
        PLANE_AXES,
        split_axis=1,
        concat_axis=1,
        tiled=True,
    )
    flattened = arrived.reshape(-1, features)
    gate_up = jnp.dot(flattened, gate_up_local, preferred_element_type=jnp.float32)
    expert_hidden = (jax.nn.silu(gate_up[:, :hidden_units]) * gate_up[:, hidden_units:]).astype(
        jnp.bfloat16
    )
    produced = jnp.dot(expert_hidden, down_local, preferred_element_type=jnp.float32).astype(
        jnp.bfloat16
    )
    returned = lax.all_to_all(
        produced.reshape(arrived.shape), PLANE_AXES, split_axis=1, concat_axis=1, tiled=True
    )
    combine = jnp.sum(jnp.where(hit, weights_all[:, None, :, :], 0.0), axis=3)
    partial = jnp.einsum(
        "hcr,hcd->hrd",
        combine,
        returned.reshape(planes, plane_slots, features).astype(jnp.float32),
        precision=lax.Precision.HIGHEST,
        preferred_element_type=jnp.float32,
    )
    mixture = lax.psum_scatter(
        partial.astype(jnp.bfloat16), "eh", scatter_dimension=0, tiled=True
    )[0].astype(jnp.float32)
    return rms_scale(hidden_state.astype(jnp.float32) + mixture, post_gain).astype(jnp.bfloat16)


def plane_split(devices):
    row = devices[0]
    try:
        coords = [tuple(d.coords) for d in row]
    except AttributeError:
        return 1, len(row)
    best = 0
    for axis in range(len(coords[0])):
        changes = [e for e in range(len(row)) if coords[e][axis] != coords[0][axis]]
        if changes:
            best = max(best, changes[0])
    if best == 0 or len(row) % best:
        return 1, len(row)
    return len(row) // best, best


def solution(mesh):
    devices = np.asarray(mesh.devices)
    planes, lanes = plane_split(devices)
    fine = Mesh(devices.reshape(devices.shape[0], planes, lanes), ROWS_AXES)
    rows = P(ROWS_AXES, None)
    placed = (
        rows,
        rows,
        P(None, "grp"),
        P(),
        P(),
        P(SLOT_AXES, None, None),
        P(SLOT_AXES, None, None),
        rows,
        rows,
        P(),
        P(ROWS_AXES),
        P(ROWS_AXES),
        P(),
        rows,
    )
    return jax.shard_map(on_device, mesh=fine, in_specs=placed, out_specs=rows, check_vma=False)
```

```python
import jax
import jax.numpy as jnp
import numpy as np
from jax import lax
from jax.sharding import Mesh
from jax.sharding import PartitionSpec as P

ROWS_AXES = ("grp", "eh", "el")
SLOT_AXES = ("eh", "el")
PLANE_AXES = ("grp", "el")


def rms_scale(values, gain):
    meansq = jnp.mean(values * values, axis=-1, keepdims=True)
    return values * lax.rsqrt(meansq + 1e-06) * gain


def on_device(
    attention,
    residual,
    out_proj,
    pre_gain,
    post_gain,
    slot_gate_up,
    slot_down,
    expert_ids,
    copy_choice,
    placement,
    request_age,
    decode_flag,
    capacity,
    route_weight,
):
    groups = lax.axis_size("grp")
    planes = lax.axis_size("eh")
    lanes = lax.axis_size("el")
    owners = planes * lanes
    devices_all = groups * owners
    rows_here = attention.shape[0]
    features = attention.shape[1]
    picks_row = expert_ids.shape[1]
    cap_size = max(2, rows_here * picks_row // devices_all)
    plane_slots = groups * lanes * cap_size
    my_plane = lax.axis_index("eh")

    columns = jnp.dot(
        lax.all_gather(attention, "grp", axis=0, tiled=True),
        out_proj,
        preferred_element_type=jnp.float32,
    )
    attn_proj = lax.all_to_all(columns, "grp", split_axis=0, concat_axis=1, tiled=True)
    hidden_state = (residual.astype(jnp.float32) + attn_proj).astype(jnp.bfloat16)
    normed = rms_scale(hidden_state.astype(jnp.float32), pre_gain).astype(jnp.bfloat16)

    experts_all = placement.shape[0]
    slot_table = jnp.arange(owners, dtype=jnp.int32)
    matches = (placement[None, :] == jnp.arange(experts_all, dtype=jnp.int32)[:, None]).astype(
        jnp.int32
    )
    slot_of = jnp.sum(slot_table[None, :] * matches, axis=1)
    expert_hits = (
        expert_ids[:, :, None] == jnp.arange(experts_all, dtype=jnp.int32)[None, None, :]
    ).astype(jnp.int32)
    slot = jnp.sum(expert_hits * slot_of[None, None, :], axis=2)
    target = copy_choice * owners + slot
    priority = decode_flag * 1048576 + request_age
    order = jnp.arange(rows_here, dtype=jnp.int32)
    ahead_mask = (priority[None, :] > priority[:, None]) | (
        priority[None, :] == priority[:, None]
    ) & (order[None, :] < order[:, None])
    target_onehot = target[:, :, None] == jnp.arange(devices_all, dtype=jnp.int32)[None, None, :]
    target_hits = jnp.sum(target_onehot.astype(jnp.bfloat16), axis=1)
    counts = jnp.dot(
        ahead_mask.astype(jnp.bfloat16), target_hits, preferred_element_type=jnp.float32
    )
    position = jnp.sum(
        jnp.where(target_onehot, counts[:, None, :], 0.0), axis=2
    ).astype(jnp.int32)
    granted = jnp.sum(
        jnp.where(target_onehot, capacity.reshape(-1)[None, None, :], 0), axis=2
    )
    accepted = position < granted
    in_plane = (copy_choice * lanes + slot % lanes) * cap_size + position
    code = jnp.where(accepted, (slot // lanes) * plane_slots + in_plane, planes * plane_slots)
    weights_kept = jnp.where(accepted, route_weight, jnp.float32(0.0))
    code_hi = (code // 128).astype(jnp.bfloat16)
    code_lo = (code % 128).astype(jnp.bfloat16)
    w_first = lax.reduce_precision(weights_kept, exponent_bits=8, mantissa_bits=7)
    w_rest = weights_kept - w_first
    w_second = lax.reduce_precision(w_rest, exponent_bits=8, mantissa_bits=7)
    w_third = w_rest - w_second
    meta = jnp.concatenate(
        [code_hi, code_lo]
        + [part.astype(jnp.bfloat16) for part in (w_first, w_second, w_third)],
        axis=1,
    )
    meta_size = rows_here * meta.shape[1]
    meta_rows = -(-meta_size // (8 * features)) * 8
    meta_block = jnp.pad(meta.reshape(-1), (0, meta_rows * features - meta_size))
    packed = jnp.concatenate([normed, meta_block.reshape(meta_rows, features)], axis=0)
    packed_all = lax.all_to_all(
        jnp.broadcast_to(packed[None], (planes,) + packed.shape), "eh", 0, 0, tiled=True
    )
    normed_all = packed_all[:, :rows_here]
    meta_all = (
        packed_all[:, rows_here:]
        .reshape(planes, -1)[:, :meta_size]
        .reshape(planes, rows_here, meta.shape[1])
        .astype(jnp.float32)
    )
    code_all = meta_all[:, :, :picks_row] * 128 + meta_all[:, :, picks_row : 2 * picks_row]
    local = code_all.astype(jnp.int32) - my_plane * plane_slots
    weights_all = (
        meta_all[:, :, 2 * picks_row : 3 * picks_row]
        + meta_all[:, :, 3 * picks_row : 4 * picks_row]
    ) + meta_all[:, :, 4 * picks_row :]
    slot_ids = jnp.arange(plane_slots, dtype=jnp.int32)
    hit = local[:, None, :, :] == slot_ids[None, :, None, None]
    dispatch = jnp.any(hit, axis=3).astype(jnp.bfloat16)
    buffer = jnp.einsum(
        "hcr,hrd->hcd", dispatch, normed_all, preferred_element_type=jnp.float32
    ).astype(jnp.bfloat16)

    gate_up_local = slot_gate_up[0]
    down_local = slot_down[0]
    hidden_units = down_local.shape[0]
    arrived = lax.all_to_all(
        buffer.reshape(planes, groups * lanes, cap_size, features),
        PLANE_AXES,
        split_axis=1,
        concat_axis=1,
        tiled=True,
    )
    flattened = arrived.reshape(-1, features)
    gate_up = jnp.dot(flattened, gate_up_local, preferred_element_type=jnp.float32)
    expert_hidden = (jax.nn.silu(gate_up[:, :hidden_units]) * gate_up[:, hidden_units:]).astype(
        jnp.bfloat16
    )
    produced = jnp.dot(expert_hidden, down_local, preferred_element_type=jnp.float32).astype(
        jnp.bfloat16
    )
    returned = lax.all_to_all(
        produced.reshape(arrived.shape), PLANE_AXES, split_axis=1, concat_axis=1, tiled=True
    )
    combine = jnp.sum(jnp.where(hit, weights_all[:, None, :, :], 0.0), axis=3)
    partial = jnp.einsum(
        "hcr,hcd->hrd",
        combine,
        returned.reshape(planes, plane_slots, features).astype(jnp.float32),
        precision=lax.Precision.HIGHEST,
        preferred_element_type=jnp.float32,
    )
    mixture = jnp.sum(
        lax.all_to_all(partial.astype(jnp.bfloat16), "eh", 0, 0, tiled=True).astype(jnp.float32),
        axis=0,
    )
    return rms_scale(hidden_state.astype(jnp.float32) + mixture, post_gain).astype(jnp.bfloat16)


def plane_split(devices):
    row = devices[0]
    try:
        coords = [tuple(d.coords) for d in row]
    except AttributeError:
        return 1, len(row)
    best = 0
    for axis in range(len(coords[0])):
        changes = [e for e in range(len(row)) if coords[e][axis] != coords[0][axis]]
        if changes:
            best = max(best, changes[0])
    if best == 0 or len(row) % best:
        return 1, len(row)
    return len(row) // best, best


def solution(mesh):
    devices = np.asarray(mesh.devices)
    planes, lanes = plane_split(devices)
    fine = Mesh(devices.reshape(devices.shape[0], planes, lanes), ROWS_AXES)
    rows = P(ROWS_AXES, None)
    placed = (
        rows,
        rows,
        P(None, "grp"),
        P(),
        P(),
        P(SLOT_AXES, None, None),
        P(SLOT_AXES, None, None),
        rows,
        rows,
        P(),
        P(ROWS_AXES),
        P(ROWS_AXES),
        P(),
        rows,
    )
    return jax.shard_map(on_device, mesh=fine, in_specs=placed, out_specs=rows, check_vma=False)
```

```python
import jax
import jax.numpy as jnp
from jax import lax
from jax.sharding import PartitionSpec as P


def rms_scale(values, gain):
    meansq = jnp.mean(values * values, axis=-1, keepdims=True)
    return values * lax.rsqrt(meansq + 1e-06) * gain


def on_device(
    attention,
    residual,
    out_proj,
    pre_gain,
    post_gain,
    slot_gate_up,
    slot_down,
    expert_ids,
    copy_choice,
    placement,
    request_age,
    decode_flag,
    capacity,
    route_weight,
):
    groups = lax.axis_size("grp")
    owners = lax.axis_size("ep")
    devices_all = groups * owners
    rows_here = attention.shape[0]
    features = attention.shape[1]
    picks_row = expert_ids.shape[1]
    cap_size = max(2, rows_here * picks_row // devices_all)
    me_grp = lax.axis_index("grp")
    blocks = [None] * groups
    blocks[0] = jnp.dot(attention, out_proj, preferred_element_type=jnp.float32)
    for shift in range(1, groups):
        ahead = [(g, (g + shift) % groups) for g in range(groups)]
        back = [(b, a) for a, b in ahead]
        visiting = lax.ppermute(attention, "grp", ahead)
        done = jnp.dot(visiting, out_proj, preferred_element_type=jnp.float32)
        blocks[shift] = lax.ppermute(done, "grp", back)
    stacked = jnp.stack(blocks, axis=0)
    order_cols = (jnp.arange(groups, dtype=jnp.int32) - me_grp) % groups
    attn_proj = jnp.concatenate(
        [jnp.take(stacked, order_cols[j], axis=0) for j in range(groups)], axis=1
    )
    hidden_state = (residual.astype(jnp.float32) + attn_proj).astype(jnp.bfloat16)
    normed = rms_scale(hidden_state.astype(jnp.float32), pre_gain).astype(jnp.bfloat16)
    experts_all = placement.shape[0]
    slot_table = jnp.arange(owners, dtype=jnp.int32)
    matches = (placement[None, :] == jnp.arange(experts_all, dtype=jnp.int32)[:, None]).astype(
        jnp.int32
    )
    slot_of = jnp.sum(slot_table[None, :] * matches, axis=1)
    expert_hits = (
        expert_ids[:, :, None] == jnp.arange(experts_all, dtype=jnp.int32)[None, None, :]
    ).astype(jnp.int32)
    target = copy_choice * owners + jnp.sum(expert_hits * slot_of[None, None, :], axis=2)
    priority = decode_flag * 1048576 + request_age
    order = jnp.arange(rows_here, dtype=jnp.int32)
    ahead_mask = (priority[None, :] > priority[:, None]) | (
        priority[None, :] == priority[:, None]
    ) & (order[None, :] < order[:, None])
    target_onehot = target[:, :, None] == jnp.arange(devices_all, dtype=jnp.int32)[None, None, :]
    target_hits = jnp.sum(target_onehot.astype(jnp.bfloat16), axis=1)
    counts = jnp.dot(
        ahead_mask.astype(jnp.bfloat16), target_hits, preferred_element_type=jnp.float32
    )
    position = jnp.sum(
        jnp.where(target_onehot, counts[:, None, :], 0.0), axis=2
    ).astype(jnp.int32)
    granted = jnp.sum(
        jnp.where(target_onehot, capacity.reshape(-1)[None, None, :], 0), axis=2
    )
    accepted = position < granted
    total_slots = devices_all * cap_size
    index = jnp.where(accepted, target * cap_size + position, total_slots)
    slot_ids = jnp.arange(total_slots, dtype=jnp.int32)
    dispatch = jnp.any(index[None, :, :] == slot_ids[:, None, None], axis=2).astype(jnp.bfloat16)
    buffer = jnp.dot(dispatch, normed, preferred_element_type=jnp.float32).astype(jnp.bfloat16)
    gate_up_local = slot_gate_up[0]
    down_local = slot_down[0]
    hidden_units = down_local.shape[0]
    arrived = lax.all_to_all(
        buffer.reshape(devices_all, cap_size, features),
        ("grp", "ep"),
        split_axis=0,
        concat_axis=0,
        tiled=True,
    )
    flattened = arrived.reshape(-1, features)
    gate_up = jnp.dot(flattened, gate_up_local, preferred_element_type=jnp.float32)
    expert_hidden = (jax.nn.silu(gate_up[:, :hidden_units]) * gate_up[:, hidden_units:]).astype(
        jnp.bfloat16
    )
    produced = jnp.dot(expert_hidden, down_local, preferred_element_type=jnp.float32).astype(
        jnp.bfloat16
    )
    returned = lax.all_to_all(
        produced.reshape(arrived.shape), ("grp", "ep"), split_axis=0, concat_axis=0, tiled=True
    )
    flat_back = returned.reshape(total_slots, features)
    weights_kept = jnp.where(accepted, route_weight, jnp.float32(0.0))
    combine = jnp.sum(
        jnp.where(index[:, :, None] == slot_ids[None, None, :], weights_kept[:, :, None], 0.0),
        axis=1,
    )
    mixture = jnp.dot(
        combine,
        flat_back.astype(jnp.float32),
        precision=lax.Precision.HIGHEST,
        preferred_element_type=jnp.float32,
    )
    return rms_scale(hidden_state.astype(jnp.float32) + mixture, post_gain).astype(jnp.bfloat16)


def solution(mesh):
    placed = (
        P(("grp", "ep"), None),
        P(("grp", "ep"), None),
        P(None, "grp"),
        P(),
        P(),
        P("ep", None, None),
        P("ep", None, None),
        P(("grp", "ep"), None),
        P(("grp", "ep"), None),
        P(),
        P(("grp", "ep")),
        P(("grp", "ep")),
        P(),
        P(("grp", "ep"), None),
    )
    return jax.shard_map(
        on_device, mesh=mesh, in_specs=placed, out_specs=P(("grp", "ep"), None), check_vma=False
    )
```

```python
import jax
import jax.numpy as jnp
from jax import lax
from jax.sharding import PartitionSpec as P


def rms_scale(values, gain):
    meansq = jnp.mean(values * values, axis=-1, keepdims=True)
    return values * lax.rsqrt(meansq + 1e-06) * gain


def on_device(
    attention,
    residual,
    out_proj,
    pre_gain,
    post_gain,
    slot_gate_up,
    slot_down,
    expert_ids,
    copy_choice,
    placement,
    request_age,
    decode_flag,
    capacity,
    route_weight,
):
    groups = lax.axis_size("grp")
    owners = lax.axis_size("ep")
    devices_all = groups * owners
    rows_here = attention.shape[0]
    features = attention.shape[1]
    picks_row = expert_ids.shape[1]
    cap_size = max(2, rows_here * picks_row // devices_all)
    me_grp = lax.axis_index("grp")
    blocks = [None] * groups
    blocks[0] = jnp.dot(attention, out_proj, preferred_element_type=jnp.float32)
    for shift in range(1, groups):
        ahead = [(g, (g + shift) % groups) for g in range(groups)]
        back = [(b, a) for a, b in ahead]
        visiting = lax.ppermute(attention, "grp", ahead)
        done = jnp.dot(visiting, out_proj, preferred_element_type=jnp.float32)
        blocks[shift] = lax.ppermute(done, "grp", back)
    stacked = jnp.stack(blocks, axis=0)
    order_cols = (jnp.arange(groups, dtype=jnp.int32) - me_grp) % groups
    attn_proj = jnp.concatenate(
        [jnp.take(stacked, order_cols[j], axis=0) for j in range(groups)], axis=1
    )
    hidden_state = (residual.astype(jnp.float32) + attn_proj).astype(jnp.bfloat16)
    normed = rms_scale(hidden_state.astype(jnp.float32), pre_gain).astype(jnp.bfloat16)
    experts_all = placement.shape[0]
    slot_table = jnp.arange(owners, dtype=jnp.int32)
    matches = (placement[None, :] == jnp.arange(experts_all, dtype=jnp.int32)[:, None]).astype(
        jnp.int32
    )
    slot_of = jnp.sum(slot_table[None, :] * matches, axis=1)
    expert_hits = (
        expert_ids[:, :, None] == jnp.arange(experts_all, dtype=jnp.int32)[None, None, :]
    ).astype(jnp.int32)
    target = copy_choice * owners + jnp.sum(expert_hits * slot_of[None, None, :], axis=2)
    priority = decode_flag * 1048576 + request_age
    order = jnp.arange(rows_here, dtype=jnp.int32)
    ahead_mask = (priority[None, :] > priority[:, None]) | (
        priority[None, :] == priority[:, None]
    ) & (order[None, :] < order[:, None])
    target_onehot = target[:, :, None] == jnp.arange(devices_all, dtype=jnp.int32)[None, None, :]
    target_hits = jnp.sum(target_onehot.astype(jnp.bfloat16), axis=1)
    counts = jnp.dot(
        ahead_mask.astype(jnp.bfloat16), target_hits, preferred_element_type=jnp.float32
    )
    position = jnp.sum(
        jnp.where(target_onehot, counts[:, None, :], 0.0), axis=2
    ).astype(jnp.int32)
    granted = jnp.sum(
        jnp.where(target_onehot, capacity.reshape(-1)[None, None, :], 0), axis=2
    )
    accepted = position < granted
    total_slots = devices_all * cap_size
    me_all = lax.axis_index(("grp", "ep"))
    index = jnp.where(
        accepted, ((target - me_all) % devices_all) * cap_size + position, total_slots
    )
    slot_ids = jnp.arange(total_slots, dtype=jnp.int32)
    dispatch = jnp.any(index[None, :, :] == slot_ids[:, None, None], axis=2).astype(jnp.bfloat16)
    buffer = jnp.dot(dispatch, normed, preferred_element_type=jnp.float32).astype(jnp.bfloat16)
    gate_up_local = slot_gate_up[0]
    down_local = slot_down[0]
    hidden_units = down_local.shape[0]
    chunks = buffer.reshape(devices_all, cap_size, features)
    arrived = jnp.stack(
        [chunks[0]]
        + [
            lax.ppermute(
                chunks[shift],
                ("grp", "ep"),
                [(i, (i + shift) % devices_all) for i in range(devices_all)],
            )
            for shift in range(1, devices_all)
        ],
        axis=0,
    )
    flattened = arrived.reshape(-1, features)
    gate_up = jnp.dot(flattened, gate_up_local, preferred_element_type=jnp.float32)
    expert_hidden = (jax.nn.silu(gate_up[:, :hidden_units]) * gate_up[:, hidden_units:]).astype(
        jnp.bfloat16
    )
    produced = jnp.dot(expert_hidden, down_local, preferred_element_type=jnp.float32).astype(
        jnp.bfloat16
    )
    outs = produced.reshape(arrived.shape)
    returned = jnp.stack(
        [outs[0]]
        + [
            lax.ppermute(
                outs[shift],
                ("grp", "ep"),
                [(i, (i - shift) % devices_all) for i in range(devices_all)],
            )
            for shift in range(1, devices_all)
        ],
        axis=0,
    )
    flat_back = returned.reshape(total_slots, features)
    weights_kept = jnp.where(accepted, route_weight, jnp.float32(0.0))
    combine = jnp.sum(
        jnp.where(index[:, :, None] == slot_ids[None, None, :], weights_kept[:, :, None], 0.0),
        axis=1,
    )
    mixture = jnp.dot(
        combine,
        flat_back.astype(jnp.float32),
        precision=lax.Precision.HIGHEST,
        preferred_element_type=jnp.float32,
    )
    return rms_scale(hidden_state.astype(jnp.float32) + mixture, post_gain).astype(jnp.bfloat16)


def solution(mesh):
    placed = (
        P(("grp", "ep"), None),
        P(("grp", "ep"), None),
        P(None, "grp"),
        P(),
        P(),
        P("ep", None, None),
        P("ep", None, None),
        P(("grp", "ep"), None),
        P(("grp", "ep"), None),
        P(),
        P(("grp", "ep")),
        P(("grp", "ep")),
        P(),
        P(("grp", "ep"), None),
    )
    return jax.shard_map(
        on_device, mesh=mesh, in_specs=placed, out_specs=P(("grp", "ep"), None), check_vma=False
    )
```

```python
import jax
import jax.numpy as jnp
import numpy as np
from jax import lax
from jax.sharding import Mesh
from jax.sharding import PartitionSpec as P

ROWS_AXES = ("grp", "eh", "el")
SLOT_AXES = ("eh", "el")
PLANE_AXES = ("grp", "el")


def rms_scale(values, gain):
    meansq = jnp.mean(values * values, axis=-1, keepdims=True)
    return values * lax.rsqrt(meansq + 1e-06) * gain


def on_device(
    attention,
    residual,
    out_proj,
    pre_gain,
    post_gain,
    slot_gate_up,
    slot_down,
    expert_ids,
    copy_choice,
    placement,
    request_age,
    decode_flag,
    capacity,
    route_weight,
):
    groups = lax.axis_size("grp")
    planes = lax.axis_size("eh")
    lanes = lax.axis_size("el")
    owners = planes * lanes
    devices_all = groups * owners
    rows_here = attention.shape[0]
    features = attention.shape[1]
    picks_row = expert_ids.shape[1]
    cap_size = max(2, rows_here * picks_row // devices_all)
    plane_slots = groups * lanes * cap_size
    my_plane = lax.axis_index("eh")

    me_grp = lax.axis_index("grp")
    blocks = [None] * groups
    blocks[0] = jnp.dot(attention, out_proj, preferred_element_type=jnp.float32)
    for shift in range(1, groups):
        ahead = [(g, (g + shift) % groups) for g in range(groups)]
        back = [(b, a) for a, b in ahead]
        visiting = lax.ppermute(attention, "grp", ahead)
        done = jnp.dot(visiting, out_proj, preferred_element_type=jnp.float32)
        blocks[shift] = lax.ppermute(done, "grp", back)
    stacked = jnp.stack(blocks, axis=0)
    order_cols = (jnp.arange(groups, dtype=jnp.int32) - me_grp) % groups
    attn_proj = jnp.concatenate(
        [jnp.take(stacked, order_cols[j], axis=0) for j in range(groups)], axis=1
    )
    hidden_state = (residual.astype(jnp.float32) + attn_proj).astype(jnp.bfloat16)
    normed = rms_scale(hidden_state.astype(jnp.float32), pre_gain).astype(jnp.bfloat16)

    experts_all = placement.shape[0]
    slot_table = jnp.arange(owners, dtype=jnp.int32)
    matches = (placement[None, :] == jnp.arange(experts_all, dtype=jnp.int32)[:, None]).astype(
        jnp.int32
    )
    slot_of = jnp.sum(slot_table[None, :] * matches, axis=1)
    expert_hits = (
        expert_ids[:, :, None] == jnp.arange(experts_all, dtype=jnp.int32)[None, None, :]
    ).astype(jnp.int32)
    slot = jnp.sum(expert_hits * slot_of[None, None, :], axis=2)
    target = copy_choice * owners + slot
    priority = decode_flag * 1048576 + request_age
    order = jnp.arange(rows_here, dtype=jnp.int32)
    ahead_mask = (priority[None, :] > priority[:, None]) | (
        priority[None, :] == priority[:, None]
    ) & (order[None, :] < order[:, None])
    target_onehot = target[:, :, None] == jnp.arange(devices_all, dtype=jnp.int32)[None, None, :]
    target_hits = jnp.sum(target_onehot.astype(jnp.bfloat16), axis=1)
    counts = jnp.dot(
        ahead_mask.astype(jnp.bfloat16), target_hits, preferred_element_type=jnp.float32
    )
    position = jnp.sum(
        jnp.where(target_onehot, counts[:, None, :], 0.0), axis=2
    ).astype(jnp.int32)
    granted = jnp.sum(
        jnp.where(target_onehot, capacity.reshape(-1)[None, None, :], 0), axis=2
    )
    accepted = position < granted
    in_plane = (copy_choice * lanes + slot % lanes) * cap_size + position
    code = jnp.where(accepted, (slot // lanes) * plane_slots + in_plane, planes * plane_slots)
    weights_kept = jnp.where(accepted, route_weight, jnp.float32(0.0))
    code_hi = (code // 128).astype(jnp.bfloat16)
    code_lo = (code % 128).astype(jnp.bfloat16)
    w_first = lax.reduce_precision(weights_kept, exponent_bits=8, mantissa_bits=7)
    w_rest = weights_kept - w_first
    w_second = lax.reduce_precision(w_rest, exponent_bits=8, mantissa_bits=7)
    w_third = w_rest - w_second
    meta = jnp.concatenate(
        [code_hi, code_lo]
        + [part.astype(jnp.bfloat16) for part in (w_first, w_second, w_third)],
        axis=1,
    )
    meta_size = rows_here * meta.shape[1]
    meta_rows = -(-meta_size // (8 * features)) * 8
    meta_block = jnp.pad(meta.reshape(-1), (0, meta_rows * features - meta_size))
    packed = jnp.concatenate([normed, meta_block.reshape(meta_rows, features)], axis=0)
    packed_all = lax.all_to_all(
        jnp.broadcast_to(packed[None], (planes,) + packed.shape), "eh", 0, 0, tiled=True
    )
    normed_all = packed_all[:, :rows_here]
    meta_all = (
        packed_all[:, rows_here:]
        .reshape(planes, -1)[:, :meta_size]
        .reshape(planes, rows_here, meta.shape[1])
        .astype(jnp.float32)
    )
    code_all = meta_all[:, :, :picks_row] * 128 + meta_all[:, :, picks_row : 2 * picks_row]
    local = code_all.astype(jnp.int32) - my_plane * plane_slots
    weights_all = (
        meta_all[:, :, 2 * picks_row : 3 * picks_row]
        + meta_all[:, :, 3 * picks_row : 4 * picks_row]
    ) + meta_all[:, :, 4 * picks_row :]
    slot_ids = jnp.arange(plane_slots, dtype=jnp.int32)
    hit = local[:, None, :, :] == slot_ids[None, :, None, None]
    dispatch = jnp.any(hit, axis=3).astype(jnp.bfloat16)
    buffer = jnp.einsum(
        "hcr,hrd->hcd", dispatch, normed_all, preferred_element_type=jnp.float32
    ).astype(jnp.bfloat16)

    gate_up_local = slot_gate_up[0]
    down_local = slot_down[0]
    hidden_units = down_local.shape[0]
    arrived = lax.all_to_all(
        buffer.reshape(planes, groups * lanes, cap_size, features),
        PLANE_AXES,
        split_axis=1,
        concat_axis=1,
        tiled=True,
    )
    flattened = arrived.reshape(-1, features)
    gate_up = jnp.dot(flattened, gate_up_local, preferred_element_type=jnp.float32)
    expert_hidden = (jax.nn.silu(gate_up[:, :hidden_units]) * gate_up[:, hidden_units:]).astype(
        jnp.bfloat16
    )
    produced = jnp.dot(expert_hidden, down_local, preferred_element_type=jnp.float32).astype(
        jnp.bfloat16
    )
    returned = lax.all_to_all(
        produced.reshape(arrived.shape), PLANE_AXES, split_axis=1, concat_axis=1, tiled=True
    )
    combine = jnp.sum(jnp.where(hit, weights_all[:, None, :, :], 0.0), axis=3)
    partial = jnp.einsum(
        "hcr,hcd->hrd",
        combine,
        returned.reshape(planes, plane_slots, features).astype(jnp.float32),
        precision=lax.Precision.HIGHEST,
        preferred_element_type=jnp.float32,
    )
    mixture = jnp.sum(
        lax.all_to_all(partial.astype(jnp.bfloat16), "eh", 0, 0, tiled=True).astype(jnp.float32),
        axis=0,
    )
    return rms_scale(hidden_state.astype(jnp.float32) + mixture, post_gain).astype(jnp.bfloat16)


def plane_split(devices):
    row = devices[0]
    try:
        coords = [tuple(d.coords) for d in row]
    except AttributeError:
        return 1, len(row)
    best = 0
    for axis in range(len(coords[0])):
        changes = [e for e in range(len(row)) if coords[e][axis] != coords[0][axis]]
        if changes:
            best = max(best, changes[0])
    if best == 0 or len(row) % best or (len(row) // best) % 2:
        return 1, len(row)
    return 2, len(row) // 2


def solution(mesh):
    devices = np.asarray(mesh.devices)
    planes, lanes = plane_split(devices)
    fine = Mesh(devices.reshape(devices.shape[0], planes, lanes), ROWS_AXES)
    rows = P(ROWS_AXES, None)
    placed = (
        rows,
        rows,
        P(None, "grp"),
        P(),
        P(),
        P(SLOT_AXES, None, None),
        P(SLOT_AXES, None, None),
        rows,
        rows,
        P(),
        P(ROWS_AXES),
        P(ROWS_AXES),
        P(),
        rows,
    )
    return jax.shard_map(on_device, mesh=fine, in_specs=placed, out_specs=rows, check_vma=False)
```

```python
import jax
import jax.numpy as jnp
import numpy as np
from jax import lax
from jax.sharding import Mesh
from jax.sharding import PartitionSpec as P

ROWS_AXES = ("grp", "eh", "el")
SLOT_AXES = ("eh", "el")
PLANE_AXES = ("grp", "el")


def rms_scale(values, gain):
    meansq = jnp.mean(values * values, axis=-1, keepdims=True)
    return values * lax.rsqrt(meansq + 1e-06) * gain


def on_device(
    attention,
    residual,
    out_proj,
    pre_gain,
    post_gain,
    slot_gate_up,
    slot_down,
    expert_ids,
    copy_choice,
    placement,
    request_age,
    decode_flag,
    capacity,
    route_weight,
):
    groups = lax.axis_size("grp")
    planes = lax.axis_size("eh")
    lanes = lax.axis_size("el")
    owners = planes * lanes
    devices_all = groups * owners
    rows_here = attention.shape[0]
    features = attention.shape[1]
    picks_row = expert_ids.shape[1]
    cap_size = max(2, rows_here * picks_row // devices_all)
    plane_slots = groups * lanes * cap_size
    my_plane = lax.axis_index("eh")

    me_grp = lax.axis_index("grp")
    blocks = [None] * groups
    blocks[0] = jnp.dot(attention, out_proj, preferred_element_type=jnp.float32)
    for shift in range(1, groups):
        ahead = [(g, (g + shift) % groups) for g in range(groups)]
        back = [(b, a) for a, b in ahead]
        visiting = lax.ppermute(attention, "grp", ahead)
        done = jnp.dot(visiting, out_proj, preferred_element_type=jnp.float32)
        blocks[shift] = lax.ppermute(done, "grp", back)
    stacked = jnp.stack(blocks, axis=0)
    order_cols = (jnp.arange(groups, dtype=jnp.int32) - me_grp) % groups
    attn_proj = jnp.concatenate(
        [jnp.take(stacked, order_cols[j], axis=0) for j in range(groups)], axis=1
    )
    hidden_state = (residual.astype(jnp.float32) + attn_proj).astype(jnp.bfloat16)
    normed = rms_scale(hidden_state.astype(jnp.float32), pre_gain).astype(jnp.bfloat16)

    experts_all = placement.shape[0]
    slot_table = jnp.arange(owners, dtype=jnp.int32)
    matches = (placement[None, :] == jnp.arange(experts_all, dtype=jnp.int32)[:, None]).astype(
        jnp.int32
    )
    slot_of = jnp.sum(slot_table[None, :] * matches, axis=1)
    expert_hits = (
        expert_ids[:, :, None] == jnp.arange(experts_all, dtype=jnp.int32)[None, None, :]
    ).astype(jnp.int32)
    slot = jnp.sum(expert_hits * slot_of[None, None, :], axis=2)
    target = copy_choice * owners + slot
    priority = decode_flag * 1048576 + request_age
    order = jnp.arange(rows_here, dtype=jnp.int32)
    ahead_mask = (priority[None, :] > priority[:, None]) | (
        priority[None, :] == priority[:, None]
    ) & (order[None, :] < order[:, None])
    target_onehot = target[:, :, None] == jnp.arange(devices_all, dtype=jnp.int32)[None, None, :]
    target_hits = jnp.sum(target_onehot.astype(jnp.bfloat16), axis=1)
    counts = jnp.dot(
        ahead_mask.astype(jnp.bfloat16), target_hits, preferred_element_type=jnp.float32
    )
    position = jnp.sum(
        jnp.where(target_onehot, counts[:, None, :], 0.0), axis=2
    ).astype(jnp.int32)
    granted = jnp.sum(
        jnp.where(target_onehot, capacity.reshape(-1)[None, None, :], 0), axis=2
    )
    accepted = position < granted
    in_plane = (copy_choice * lanes + slot % lanes) * cap_size + position
    code = jnp.where(accepted, (slot // lanes) * plane_slots + in_plane, planes * plane_slots)
    weights_kept = jnp.where(accepted, route_weight, jnp.float32(0.0))
    code_hi = (code // 128).astype(jnp.bfloat16)
    code_lo = (code % 128).astype(jnp.bfloat16)
    w_first = lax.reduce_precision(weights_kept, exponent_bits=8, mantissa_bits=7)
    w_rest = weights_kept - w_first
    w_second = lax.reduce_precision(w_rest, exponent_bits=8, mantissa_bits=7)
    w_third = w_rest - w_second
    meta = jnp.concatenate(
        [code_hi, code_lo]
        + [part.astype(jnp.bfloat16) for part in (w_first, w_second, w_third)],
        axis=1,
    )
    meta_size = rows_here * meta.shape[1]
    meta_rows = -(-meta_size // (8 * features)) * 8
    meta_block = jnp.pad(meta.reshape(-1), (0, meta_rows * features - meta_size))
    packed = jnp.concatenate([normed, meta_block.reshape(meta_rows, features)], axis=0)
    gate_up_local = slot_gate_up[0]
    down_local = slot_down[0]
    hidden_units = down_local.shape[0]
    slot_ids = jnp.arange(plane_slots, dtype=jnp.int32)

    def expert(rows_in):
        gate_up = jnp.dot(rows_in, gate_up_local, preferred_element_type=jnp.float32)
        expert_hidden = (
            jax.nn.silu(gate_up[:, :hidden_units]) * gate_up[:, hidden_units:]
        ).astype(jnp.bfloat16)
        return jnp.dot(expert_hidden, down_local, preferred_element_type=jnp.float32).astype(
            jnp.bfloat16
        )

    received = [packed] + [
        lax.ppermute(packed, "eh", [(i, (i + shift) % planes) for i in range(planes)])
        for shift in range(1, planes)
    ]
    partials = []
    for shift, block in enumerate(received):
        normed_s = block[:rows_here]
        meta_s = (
            block[rows_here:]
            .reshape(-1)[:meta_size]
            .reshape(rows_here, meta.shape[1])
            .astype(jnp.float32)
        )
        code_s = meta_s[:, :picks_row] * 128 + meta_s[:, picks_row : 2 * picks_row]
        local = code_s.astype(jnp.int32) - my_plane * plane_slots
        weights_s = (
            meta_s[:, 2 * picks_row : 3 * picks_row] + meta_s[:, 3 * picks_row : 4 * picks_row]
        ) + meta_s[:, 4 * picks_row :]
        hit = local[None, :, :] == slot_ids[:, None, None]
        dispatch = jnp.any(hit, axis=2).astype(jnp.bfloat16)
        buffer = jnp.dot(dispatch, normed_s, preferred_element_type=jnp.float32).astype(
            jnp.bfloat16
        )
        arrived = lax.all_to_all(
            buffer.reshape(groups * lanes, cap_size, features),
            PLANE_AXES,
            split_axis=0,
            concat_axis=0,
            tiled=True,
        )
        produced = expert(arrived.reshape(-1, features))
        returned = lax.all_to_all(
            produced.reshape(arrived.shape), PLANE_AXES, split_axis=0, concat_axis=0, tiled=True
        )
        combine = jnp.sum(jnp.where(hit, weights_s[None, :, :], 0.0), axis=2)
        partial = jnp.dot(
            combine.T,
            returned.reshape(plane_slots, features).astype(jnp.float32),
            precision=lax.Precision.HIGHEST,
            preferred_element_type=jnp.float32,
        )
        if shift:
            back = [((i + shift) % planes, i) for i in range(planes)]
            partial = lax.ppermute(partial.astype(jnp.bfloat16), "eh", back).astype(jnp.float32)
        partials.append(partial)
    mixture = partials[0]
    for partial in partials[1:]:
        mixture = mixture + partial
    return rms_scale(hidden_state.astype(jnp.float32) + mixture, post_gain).astype(jnp.bfloat16)


def plane_split(devices):
    row = devices[0]
    try:
        coords = [tuple(d.coords) for d in row]
    except AttributeError:
        return 1, len(row)
    best = 0
    for axis in range(len(coords[0])):
        changes = [e for e in range(len(row)) if coords[e][axis] != coords[0][axis]]
        if changes:
            best = max(best, changes[0])
    if best == 0 or len(row) % best or (len(row) // best) % 2:
        return 1, len(row)
    return 2, len(row) // 2


def solution(mesh):
    devices = np.asarray(mesh.devices)
    planes, lanes = plane_split(devices)
    fine = Mesh(devices.reshape(devices.shape[0], planes, lanes), ROWS_AXES)
    rows = P(ROWS_AXES, None)
    placed = (
        rows,
        rows,
        P(None, "grp"),
        P(),
        P(),
        P(SLOT_AXES, None, None),
        P(SLOT_AXES, None, None),
        rows,
        rows,
        P(),
        P(ROWS_AXES),
        P(ROWS_AXES),
        P(),
        rows,
    )
    return jax.shard_map(on_device, mesh=fine, in_specs=placed, out_specs=rows, check_vma=False)
```

```python
import jax
import jax.numpy as jnp
import numpy as np
from jax import lax
from jax.sharding import Mesh
from jax.sharding import PartitionSpec as P

ROWS_AXES = ("grp", "eh", "el")
SLOT_AXES = ("eh", "el")
PLANE_AXES = ("grp", "el")


def rms_scale(values, gain):
    meansq = jnp.mean(values * values, axis=-1, keepdims=True)
    return values * lax.rsqrt(meansq + 1e-06) * gain


def on_device(
    attention,
    residual,
    out_proj,
    pre_gain,
    post_gain,
    slot_gate_up,
    slot_down,
    expert_ids,
    copy_choice,
    placement,
    request_age,
    decode_flag,
    capacity,
    route_weight,
):
    groups = lax.axis_size("grp")
    planes = lax.axis_size("eh")
    lanes = lax.axis_size("el")
    owners = planes * lanes
    devices_all = groups * owners
    rows_here = attention.shape[0]
    features = attention.shape[1]
    picks_row = expert_ids.shape[1]
    cap_size = max(2, rows_here * picks_row // devices_all)
    plane_slots = groups * lanes * cap_size
    my_plane = lax.axis_index("eh")

    me_grp = lax.axis_index("grp")
    blocks = [None] * groups
    blocks[0] = jnp.dot(attention, out_proj, preferred_element_type=jnp.float32)
    for shift in range(1, groups):
        ahead = [(g, (g + shift) % groups) for g in range(groups)]
        back = [(b, a) for a, b in ahead]
        visiting = lax.ppermute(attention, "grp", ahead)
        done = jnp.dot(visiting, out_proj, preferred_element_type=jnp.float32)
        blocks[shift] = lax.ppermute(done, "grp", back)
    stacked = jnp.stack(blocks, axis=0)
    order_cols = (jnp.arange(groups, dtype=jnp.int32) - me_grp) % groups
    attn_proj = jnp.concatenate(
        [jnp.take(stacked, order_cols[j], axis=0) for j in range(groups)], axis=1
    )
    hidden_state = (residual.astype(jnp.float32) + attn_proj).astype(jnp.bfloat16)
    normed = rms_scale(hidden_state.astype(jnp.float32), pre_gain).astype(jnp.bfloat16)

    experts_all = placement.shape[0]
    slot_table = jnp.arange(owners, dtype=jnp.int32)
    matches = (placement[None, :] == jnp.arange(experts_all, dtype=jnp.int32)[:, None]).astype(
        jnp.int32
    )
    slot_of = jnp.sum(slot_table[None, :] * matches, axis=1)
    expert_hits = (
        expert_ids[:, :, None] == jnp.arange(experts_all, dtype=jnp.int32)[None, None, :]
    ).astype(jnp.int32)
    slot = jnp.sum(expert_hits * slot_of[None, None, :], axis=2)
    target = copy_choice * owners + slot
    priority = decode_flag * 1048576 + request_age
    order = jnp.arange(rows_here, dtype=jnp.int32)
    ahead_mask = (priority[None, :] > priority[:, None]) | (
        priority[None, :] == priority[:, None]
    ) & (order[None, :] < order[:, None])
    target_onehot = target[:, :, None] == jnp.arange(devices_all, dtype=jnp.int32)[None, None, :]
    target_hits = jnp.sum(target_onehot.astype(jnp.bfloat16), axis=1)
    counts = jnp.dot(
        ahead_mask.astype(jnp.bfloat16), target_hits, preferred_element_type=jnp.float32
    )
    position = jnp.sum(
        jnp.where(target_onehot, counts[:, None, :], 0.0), axis=2
    ).astype(jnp.int32)
    granted = jnp.sum(
        jnp.where(target_onehot, capacity.reshape(-1)[None, None, :], 0), axis=2
    )
    accepted = position < granted
    in_plane = (copy_choice * lanes + slot % lanes) * cap_size + position
    code = jnp.where(accepted, (slot // lanes) * plane_slots + in_plane, planes * plane_slots)
    weights_kept = jnp.where(accepted, route_weight, jnp.float32(0.0))
    code_hi = (code // 128).astype(jnp.bfloat16)
    code_lo = (code % 128).astype(jnp.bfloat16)
    w_first = lax.reduce_precision(weights_kept, exponent_bits=8, mantissa_bits=7)
    w_rest = weights_kept - w_first
    w_second = lax.reduce_precision(w_rest, exponent_bits=8, mantissa_bits=7)
    w_third = w_rest - w_second
    meta = jnp.concatenate(
        [code_hi, code_lo]
        + [part.astype(jnp.bfloat16) for part in (w_first, w_second, w_third)],
        axis=1,
    )
    meta_size = rows_here * meta.shape[1]
    meta_rows = -(-meta_size // (8 * features)) * 8
    meta_block = jnp.pad(meta.reshape(-1), (0, meta_rows * features - meta_size))
    packed = jnp.concatenate([normed, meta_block.reshape(meta_rows, features)], axis=0)
    gate_up_local = slot_gate_up[0]
    down_local = slot_down[0]
    hidden_units = down_local.shape[0]
    slot_ids = jnp.arange(plane_slots, dtype=jnp.int32)

    def expert(rows_in):
        gate_up = jnp.dot(rows_in, gate_up_local, preferred_element_type=jnp.float32)
        expert_hidden = (
            jax.nn.silu(gate_up[:, :hidden_units]) * gate_up[:, hidden_units:]
        ).astype(jnp.bfloat16)
        return jnp.dot(expert_hidden, down_local, preferred_element_type=jnp.float32).astype(
            jnp.bfloat16
        )

    received = [packed] + [
        lax.ppermute(packed, "eh", [(i, (i + shift) % planes) for i in range(planes)])
        for shift in range(1, planes)
    ]
    partials = []
    for shift, block in enumerate(received):
        if shift:
            block = block + jnp.zeros_like(block) * first_arrived
        normed_s = block[:rows_here]
        meta_s = (
            block[rows_here:]
            .reshape(-1)[:meta_size]
            .reshape(rows_here, meta.shape[1])
            .astype(jnp.float32)
        )
        code_s = meta_s[:, :picks_row] * 128 + meta_s[:, picks_row : 2 * picks_row]
        local = code_s.astype(jnp.int32) - my_plane * plane_slots
        weights_s = (
            meta_s[:, 2 * picks_row : 3 * picks_row] + meta_s[:, 3 * picks_row : 4 * picks_row]
        ) + meta_s[:, 4 * picks_row :]
        hit = local[None, :, :] == slot_ids[:, None, None]
        dispatch = jnp.any(hit, axis=2).astype(jnp.bfloat16)
        buffer = jnp.dot(dispatch, normed_s, preferred_element_type=jnp.float32).astype(
            jnp.bfloat16
        )
        arrived = lax.all_to_all(
            buffer.reshape(groups * lanes, cap_size, features),
            PLANE_AXES,
            split_axis=0,
            concat_axis=0,
            tiled=True,
        )
        if shift == 0:
            first_arrived = arrived[:1, 0, :1]
        produced = expert(arrived.reshape(-1, features))
        returned = lax.all_to_all(
            produced.reshape(arrived.shape), PLANE_AXES, split_axis=0, concat_axis=0, tiled=True
        )
        combine = jnp.sum(jnp.where(hit, weights_s[None, :, :], 0.0), axis=2)
        partial = jnp.dot(
            combine.T,
            returned.reshape(plane_slots, features).astype(jnp.float32),
            precision=lax.Precision.HIGHEST,
            preferred_element_type=jnp.float32,
        )
        if shift:
            back = [((i + shift) % planes, i) for i in range(planes)]
            partial = lax.ppermute(partial.astype(jnp.bfloat16), "eh", back).astype(jnp.float32)
        partials.append(partial)
    mixture = partials[0]
    for partial in partials[1:]:
        mixture = mixture + partial
    return rms_scale(hidden_state.astype(jnp.float32) + mixture, post_gain).astype(jnp.bfloat16)


def plane_split(devices):
    row = devices[0]
    try:
        coords = [tuple(d.coords) for d in row]
    except AttributeError:
        return 1, len(row)
    best = 0
    for axis in range(len(coords[0])):
        changes = [e for e in range(len(row)) if coords[e][axis] != coords[0][axis]]
        if changes:
            best = max(best, changes[0])
    if best == 0 or len(row) % best or (len(row) // best) % 2:
        return 1, len(row)
    return 2, len(row) // 2


def solution(mesh):
    devices = np.asarray(mesh.devices)
    planes, lanes = plane_split(devices)
    fine = Mesh(devices.reshape(devices.shape[0], planes, lanes), ROWS_AXES)
    rows = P(ROWS_AXES, None)
    placed = (
        rows,
        rows,
        P(None, "grp"),
        P(),
        P(),
        P(SLOT_AXES, None, None),
        P(SLOT_AXES, None, None),
        rows,
        rows,
        P(),
        P(ROWS_AXES),
        P(ROWS_AXES),
        P(),
        rows,
    )
    return jax.shard_map(on_device, mesh=fine, in_specs=placed, out_specs=rows, check_vma=False)
```

```python
import jax
import jax.numpy as jnp
import numpy as np
from jax import lax
from jax.sharding import Mesh
from jax.sharding import PartitionSpec as P

ROWS_AXES = ("grp", "eh", "el")
SLOT_AXES = ("eh", "el")
PLANE_AXES = ("grp", "el")


def rms_scale(values, gain):
    meansq = jnp.mean(values * values, axis=-1, keepdims=True)
    return values * lax.rsqrt(meansq + 1e-06) * gain


def on_device(
    attention,
    residual,
    out_proj,
    pre_gain,
    post_gain,
    slot_gate_up,
    slot_down,
    expert_ids,
    copy_choice,
    placement,
    request_age,
    decode_flag,
    capacity,
    route_weight,
):
    groups = lax.axis_size("grp")
    planes = lax.axis_size("eh")
    lanes = lax.axis_size("el")
    owners = planes * lanes
    devices_all = groups * owners
    rows_here = attention.shape[0]
    features = attention.shape[1]
    picks_row = expert_ids.shape[1]
    cap_size = max(2, rows_here * picks_row // devices_all)
    plane_slots = groups * lanes * cap_size
    my_plane = lax.axis_index("eh")

    me_grp = lax.axis_index("grp")
    blocks = [None] * groups
    blocks[0] = jnp.dot(attention, out_proj, preferred_element_type=jnp.float32)
    for shift in range(1, groups):
        ahead = [(g, (g + shift) % groups) for g in range(groups)]
        back = [(b, a) for a, b in ahead]
        visiting = lax.ppermute(attention, "grp", ahead)
        done = jnp.dot(visiting, out_proj, preferred_element_type=jnp.float32)
        blocks[shift] = lax.ppermute(done, "grp", back)
    stacked = jnp.stack(blocks, axis=0)
    order_cols = (jnp.arange(groups, dtype=jnp.int32) - me_grp) % groups
    attn_proj = jnp.concatenate(
        [jnp.take(stacked, order_cols[j], axis=0) for j in range(groups)], axis=1
    )
    hidden_state = (residual.astype(jnp.float32) + attn_proj).astype(jnp.bfloat16)
    normed = rms_scale(hidden_state.astype(jnp.float32), pre_gain).astype(jnp.bfloat16)

    experts_all = placement.shape[0]
    slot_table = jnp.arange(owners, dtype=jnp.int32)
    matches = (placement[None, :] == jnp.arange(experts_all, dtype=jnp.int32)[:, None]).astype(
        jnp.int32
    )
    slot_of = jnp.sum(slot_table[None, :] * matches, axis=1)
    expert_hits = (
        expert_ids[:, :, None] == jnp.arange(experts_all, dtype=jnp.int32)[None, None, :]
    ).astype(jnp.int32)
    slot = jnp.sum(expert_hits * slot_of[None, None, :], axis=2)
    target = copy_choice * owners + slot
    priority = decode_flag * 1048576 + request_age
    order = jnp.arange(rows_here, dtype=jnp.int32)
    ahead_mask = (priority[None, :] > priority[:, None]) | (
        priority[None, :] == priority[:, None]
    ) & (order[None, :] < order[:, None])
    target_onehot = target[:, :, None] == jnp.arange(devices_all, dtype=jnp.int32)[None, None, :]
    target_hits = jnp.sum(target_onehot.astype(jnp.bfloat16), axis=1)
    counts = jnp.dot(
        ahead_mask.astype(jnp.bfloat16), target_hits, preferred_element_type=jnp.float32
    )
    position = jnp.sum(
        jnp.where(target_onehot, counts[:, None, :], 0.0), axis=2
    ).astype(jnp.int32)
    granted = jnp.sum(
        jnp.where(target_onehot, capacity.reshape(-1)[None, None, :], 0), axis=2
    )
    accepted = position < granted
    in_plane = (copy_choice * lanes + slot % lanes) * cap_size + position
    code = jnp.where(accepted, (slot // lanes) * plane_slots + in_plane, planes * plane_slots)
    weights_kept = jnp.where(accepted, route_weight, jnp.float32(0.0))
    code_hi = (code // 128).astype(jnp.bfloat16)
    code_lo = (code % 128).astype(jnp.bfloat16)
    w_first = lax.reduce_precision(weights_kept, exponent_bits=8, mantissa_bits=7)
    w_rest = weights_kept - w_first
    w_second = lax.reduce_precision(w_rest, exponent_bits=8, mantissa_bits=7)
    w_third = w_rest - w_second
    meta = jnp.concatenate(
        [code_hi, code_lo]
        + [part.astype(jnp.bfloat16) for part in (w_first, w_second, w_third)],
        axis=1,
    )
    meta_size = rows_here * meta.shape[1]
    meta_rows = -(-meta_size // (8 * features)) * 8
    meta_block = jnp.pad(meta.reshape(-1), (0, meta_rows * features - meta_size))
    packed = jnp.concatenate([normed, meta_block.reshape(meta_rows, features)], axis=0)
    gate_up_local = slot_gate_up[0]
    down_local = slot_down[0]
    hidden_units = down_local.shape[0]
    slot_ids = jnp.arange(plane_slots, dtype=jnp.int32)

    def expert(rows_in):
        gate_up = jnp.dot(rows_in, gate_up_local, preferred_element_type=jnp.float32)
        expert_hidden = (
            jax.nn.silu(gate_up[:, :hidden_units]) * gate_up[:, hidden_units:]
        ).astype(jnp.bfloat16)
        return jnp.dot(expert_hidden, down_local, preferred_element_type=jnp.float32).astype(
            jnp.bfloat16
        )

    received = [packed] + [
        lax.ppermute(packed, "eh", [(i, (i + shift) % planes) for i in range(planes)])
        for shift in range(1, planes)
    ]
    partials = []
    for shift, block in enumerate(received):
        if shift:
            block = block + jnp.zeros_like(block) * first_arrived
        normed_s = block[:rows_here]
        meta_s = (
            block[rows_here:]
            .reshape(-1)[:meta_size]
            .reshape(rows_here, meta.shape[1])
            .astype(jnp.float32)
        )
        code_s = meta_s[:, :picks_row] * 128 + meta_s[:, picks_row : 2 * picks_row]
        local = code_s.astype(jnp.int32) - my_plane * plane_slots
        hit = local[None, :, :] == slot_ids[:, None, None]
        dispatch = jnp.any(hit, axis=2).astype(jnp.bfloat16)
        buffer = jnp.dot(dispatch, normed_s, preferred_element_type=jnp.float32).astype(
            jnp.bfloat16
        )
        arrived = lax.all_to_all(
            buffer.reshape(groups * lanes, cap_size, features),
            PLANE_AXES,
            split_axis=0,
            concat_axis=0,
            tiled=True,
        )
        if shift == 0:
            first_arrived = arrived[:1, 0, :1]
        produced = expert(arrived.reshape(-1, features))
        returned = lax.all_to_all(
            produced.reshape(arrived.shape), PLANE_AXES, split_axis=0, concat_axis=0, tiled=True
        )
        parts = [
            jnp.sum(jnp.where(hit, meta_s[None, :, k0 : k0 + picks_row], 0.0), axis=2)
            for k0 in range(2 * picks_row, 5 * picks_row, picks_row)
        ]
        stacked = jnp.concatenate([p.T for p in parts], axis=0).astype(jnp.bfloat16)
        products = jnp.dot(
            stacked,
            returned.reshape(plane_slots, features),
            preferred_element_type=jnp.float32,
        )
        partial = (
            products[:rows_here] + products[rows_here : 2 * rows_here]
        ) + products[2 * rows_here :]
        if shift:
            back = [((i + shift) % planes, i) for i in range(planes)]
            partial = lax.ppermute(partial.astype(jnp.bfloat16), "eh", back).astype(jnp.float32)
        partials.append(partial)
    mixture = partials[0]
    for partial in partials[1:]:
        mixture = mixture + partial
    return rms_scale(hidden_state.astype(jnp.float32) + mixture, post_gain).astype(jnp.bfloat16)


def plane_split(devices):
    row = devices[0]
    try:
        coords = [tuple(d.coords) for d in row]
    except AttributeError:
        return 1, len(row)
    best = 0
    for axis in range(len(coords[0])):
        changes = [e for e in range(len(row)) if coords[e][axis] != coords[0][axis]]
        if changes:
            best = max(best, changes[0])
    if best == 0 or len(row) % best or (len(row) // best) % 2:
        return 1, len(row)
    return 2, len(row) // 2


def solution(mesh):
    devices = np.asarray(mesh.devices)
    planes, lanes = plane_split(devices)
    fine = Mesh(devices.reshape(devices.shape[0], planes, lanes), ROWS_AXES)
    rows = P(ROWS_AXES, None)
    placed = (
        rows,
        rows,
        P(None, "grp"),
        P(),
        P(),
        P(SLOT_AXES, None, None),
        P(SLOT_AXES, None, None),
        rows,
        rows,
        P(),
        P(ROWS_AXES),
        P(ROWS_AXES),
        P(),
        rows,
    )
    return jax.shard_map(on_device, mesh=fine, in_specs=placed, out_specs=rows, check_vma=False)
```

```python
import jax
import jax.numpy as jnp
import numpy as np
from jax import lax
from jax.sharding import Mesh
from jax.sharding import PartitionSpec as P

ROWS_AXES = ("grp", "eh", "el")
SLOT_AXES = ("eh", "el")
PLANE_AXES = ("grp", "el")


def rms_scale(values, gain):
    meansq = jnp.mean(values * values, axis=-1, keepdims=True)
    return values * lax.rsqrt(meansq + 1e-06) * gain


def on_device(
    attention,
    residual,
    out_proj,
    pre_gain,
    post_gain,
    slot_gate_up,
    slot_down,
    expert_ids,
    copy_choice,
    placement,
    request_age,
    decode_flag,
    capacity,
    route_weight,
):
    groups = lax.axis_size("grp")
    planes = lax.axis_size("eh")
    lanes = lax.axis_size("el")
    owners = planes * lanes
    devices_all = groups * owners
    rows_here = attention.shape[0]
    features = attention.shape[1]
    picks_row = expert_ids.shape[1]
    cap_size = max(2, rows_here * picks_row // devices_all)
    plane_slots = groups * lanes * cap_size
    my_plane = lax.axis_index("eh")

    me_grp = lax.axis_index("grp")
    pair = jnp.concatenate([attention, residual], axis=0)
    pairs_in = [pair] + [
        lax.ppermute(pair, "eh", [(i, (i + shift) % planes) for i in range(planes)])
        for shift in range(1, planes)
    ]
    cols = [[jnp.dot(p[:rows_here], out_proj, preferred_element_type=jnp.float32)]
            for p in pairs_in]
    for shift in range(1, groups):
        ahead = [(g, (g + shift) % groups) for g in range(groups)]
        visiting = lax.ppermute(attention, "grp", ahead)
        done = jnp.dot(visiting, out_proj, preferred_element_type=jnp.float32)
        for plane_shift in range(planes):
            sends = [
                (
                    g * planes + h,
                    ((g - shift) % groups) * planes + (h + plane_shift) % planes,
                )
                for g in range(groups)
                for h in range(planes)
            ]
            cols[plane_shift].append(lax.ppermute(done, ("grp", "eh"), sends))
    order_cols = (jnp.arange(groups, dtype=jnp.int32) - me_grp) % groups
    normed_in = []
    for plane_shift in range(planes):
        stacked = jnp.stack(cols[plane_shift], axis=0)
        attn_proj = jnp.concatenate(
            [jnp.take(stacked, order_cols[j], axis=0) for j in range(groups)], axis=1
        )
        residual_s = pairs_in[plane_shift][rows_here:]
        hidden_s = (residual_s.astype(jnp.float32) + attn_proj).astype(jnp.bfloat16)
        if plane_shift == 0:
            hidden_state = hidden_s
        normed_in.append(
            rms_scale(hidden_s.astype(jnp.float32), pre_gain).astype(jnp.bfloat16)
        )

    experts_all = placement.shape[0]
    slot_table = jnp.arange(owners, dtype=jnp.int32)
    matches = (placement[None, :] == jnp.arange(experts_all, dtype=jnp.int32)[:, None]).astype(
        jnp.int32
    )
    slot_of = jnp.sum(slot_table[None, :] * matches, axis=1)
    expert_hits = (
        expert_ids[:, :, None] == jnp.arange(experts_all, dtype=jnp.int32)[None, None, :]
    ).astype(jnp.int32)
    slot = jnp.sum(expert_hits * slot_of[None, None, :], axis=2)
    target = copy_choice * owners + slot
    priority = decode_flag * 1048576 + request_age
    order = jnp.arange(rows_here, dtype=jnp.int32)
    ahead_mask = (priority[None, :] > priority[:, None]) | (
        priority[None, :] == priority[:, None]
    ) & (order[None, :] < order[:, None])
    target_onehot = target[:, :, None] == jnp.arange(devices_all, dtype=jnp.int32)[None, None, :]
    target_hits = jnp.sum(target_onehot.astype(jnp.bfloat16), axis=1)
    counts = jnp.dot(
        ahead_mask.astype(jnp.bfloat16), target_hits, preferred_element_type=jnp.float32
    )
    position = jnp.sum(
        jnp.where(target_onehot, counts[:, None, :], 0.0), axis=2
    ).astype(jnp.int32)
    granted = jnp.sum(
        jnp.where(target_onehot, capacity.reshape(-1)[None, None, :], 0), axis=2
    )
    accepted = position < granted
    in_plane = (copy_choice * lanes + slot % lanes) * cap_size + position
    code = jnp.where(accepted, (slot // lanes) * plane_slots + in_plane, planes * plane_slots)
    weights_kept = jnp.where(accepted, route_weight, jnp.float32(0.0))
    code_hi = (code // 128).astype(jnp.bfloat16)
    code_lo = (code % 128).astype(jnp.bfloat16)
    w_first = lax.reduce_precision(weights_kept, exponent_bits=8, mantissa_bits=7)
    w_rest = weights_kept - w_first
    w_second = lax.reduce_precision(w_rest, exponent_bits=8, mantissa_bits=7)
    w_third = w_rest - w_second
    meta = jnp.concatenate(
        [code_hi, code_lo]
        + [part.astype(jnp.bfloat16) for part in (w_first, w_second, w_third)],
        axis=1,
    )
    meta_size = rows_here * meta.shape[1]
    meta_rows = -(-meta_size // (8 * features)) * 8
    meta_block = jnp.pad(meta.reshape(-1), (0, meta_rows * features - meta_size))
    meta_block = meta_block.reshape(meta_rows, features)
    meta_in = [meta_block] + [
        lax.ppermute(meta_block, "eh", [(i, (i + shift) % planes) for i in range(planes)])
        for shift in range(1, planes)
    ]
    gate_up_local = slot_gate_up[0]
    down_local = slot_down[0]
    hidden_units = down_local.shape[0]
    slot_ids = jnp.arange(plane_slots, dtype=jnp.int32)

    def expert(rows_in):
        gate_up = jnp.dot(rows_in, gate_up_local, preferred_element_type=jnp.float32)
        expert_hidden = (
            jax.nn.silu(gate_up[:, :hidden_units]) * gate_up[:, hidden_units:]
        ).astype(jnp.bfloat16)
        return jnp.dot(expert_hidden, down_local, preferred_element_type=jnp.float32).astype(
            jnp.bfloat16
        )

    hits = []
    weights_in = []
    buffers = []
    for shift in range(planes):
        meta_s = (
            meta_in[shift]
            .reshape(-1)[:meta_size]
            .reshape(rows_here, meta.shape[1])
            .astype(jnp.float32)
        )
        code_s = meta_s[:, :picks_row] * 128 + meta_s[:, picks_row : 2 * picks_row]
        local = code_s.astype(jnp.int32) - my_plane * plane_slots
        weights_in.append(
            (meta_s[:, 2 * picks_row : 3 * picks_row] + meta_s[:, 3 * picks_row : 4 * picks_row])
            + meta_s[:, 4 * picks_row :]
        )
        hit = local[None, :, :] == slot_ids[:, None, None]
        hits.append(hit)
        dispatch = jnp.any(hit, axis=2).astype(jnp.bfloat16)
        buffer = jnp.dot(dispatch, normed_in[shift], preferred_element_type=jnp.float32)
        buffers.append(buffer.astype(jnp.bfloat16).reshape(groups * lanes, cap_size, features))
    arrived = lax.all_to_all(
        jnp.stack(buffers, axis=1), PLANE_AXES, split_axis=0, concat_axis=0, tiled=True
    )
    produced = expert(arrived.reshape(-1, features)).reshape(arrived.shape)
    partials = [None] * planes
    for shift in list(range(1, planes)) + [0]:
        returned = lax.all_to_all(
            produced[:, shift], PLANE_AXES, split_axis=0, concat_axis=0, tiled=True
        )
        combine = jnp.sum(jnp.where(hits[shift], weights_in[shift][None, :, :], 0.0), axis=2)
        partial = jnp.dot(
            combine.T,
            returned.reshape(plane_slots, features).astype(jnp.float32),
            precision=lax.Precision.HIGHEST,
            preferred_element_type=jnp.float32,
        )
        if shift:
            back = [((i + shift) % planes, i) for i in range(planes)]
            partial = lax.ppermute(partial.astype(jnp.bfloat16), "eh", back).astype(jnp.float32)
        partials[shift] = partial
    mixture = partials[0]
    for partial in partials[1:]:
        mixture = mixture + partial
    return rms_scale(hidden_state.astype(jnp.float32) + mixture, post_gain).astype(jnp.bfloat16)


def plane_split(devices):
    row = devices[0]
    try:
        coords = [tuple(d.coords) for d in row]
    except AttributeError:
        return 1, len(row)
    best = 0
    for axis in range(len(coords[0])):
        changes = [e for e in range(len(row)) if coords[e][axis] != coords[0][axis]]
        if changes:
            best = max(best, changes[0])
    if best == 0 or len(row) % best or (len(row) // best) % 2:
        return 1, len(row)
    return 2, len(row) // 2


def solution(mesh):
    devices = np.asarray(mesh.devices)
    planes, lanes = plane_split(devices)
    fine = Mesh(devices.reshape(devices.shape[0], planes, lanes), ROWS_AXES)
    rows = P(ROWS_AXES, None)
    placed = (
        rows,
        rows,
        P(None, "grp"),
        P(),
        P(),
        P(SLOT_AXES, None, None),
        P(SLOT_AXES, None, None),
        rows,
        rows,
        P(),
        P(ROWS_AXES),
        P(ROWS_AXES),
        P(),
        rows,
    )
    return jax.shard_map(on_device, mesh=fine, in_specs=placed, out_specs=rows, check_vma=False)
```

```python
import jax
import jax.numpy as jnp
import numpy as np
from jax import lax
from jax.sharding import Mesh
from jax.sharding import PartitionSpec as P

ROWS_AXES = ("grp", "eh", "el")
SLOT_AXES = ("eh", "el")
PLANE_AXES = ("grp", "el")


def rms_scale(values, gain):
    meansq = jnp.mean(values * values, axis=-1, keepdims=True)
    return values * lax.rsqrt(meansq + 1e-06) * gain


def on_device(
    attention,
    residual,
    out_proj,
    pre_gain,
    post_gain,
    slot_gate_up,
    slot_down,
    expert_ids,
    copy_choice,
    placement,
    request_age,
    decode_flag,
    capacity,
    route_weight,
):
    groups = lax.axis_size("grp")
    planes = lax.axis_size("eh")
    lanes = lax.axis_size("el")
    owners = planes * lanes
    devices_all = groups * owners
    rows_here = attention.shape[0]
    features = attention.shape[1]
    picks_row = expert_ids.shape[1]
    cap_size = max(2, rows_here * picks_row // devices_all)
    plane_slots = groups * lanes * cap_size
    my_plane = lax.axis_index("eh")

    me_grp = lax.axis_index("grp")
    blocks = [None] * groups
    blocks[0] = jnp.dot(attention, out_proj, preferred_element_type=jnp.float32)
    for shift in range(1, groups):
        ahead = [(g, (g + shift) % groups) for g in range(groups)]
        back = [(b, a) for a, b in ahead]
        visiting = lax.ppermute(attention, "grp", ahead)
        done = jnp.dot(visiting, out_proj, preferred_element_type=jnp.float32)
        blocks[shift] = lax.ppermute(done, "grp", back)
    stacked = jnp.stack(blocks, axis=0)
    order_cols = (jnp.arange(groups, dtype=jnp.int32) - me_grp) % groups
    attn_proj = jnp.concatenate(
        [jnp.take(stacked, order_cols[j], axis=0) for j in range(groups)], axis=1
    )
    hidden_state = (residual.astype(jnp.float32) + attn_proj).astype(jnp.bfloat16)
    normed = rms_scale(hidden_state.astype(jnp.float32), pre_gain).astype(jnp.bfloat16)

    experts_all = placement.shape[0]
    slot_table = jnp.arange(owners, dtype=jnp.int32)
    matches = (placement[None, :] == jnp.arange(experts_all, dtype=jnp.int32)[:, None]).astype(
        jnp.int32
    )
    slot_of = jnp.sum(slot_table[None, :] * matches, axis=1)
    expert_hits = (
        expert_ids[:, :, None] == jnp.arange(experts_all, dtype=jnp.int32)[None, None, :]
    ).astype(jnp.int32)
    slot = jnp.sum(expert_hits * slot_of[None, None, :], axis=2)
    target = copy_choice * owners + slot
    priority = decode_flag * 1048576 + request_age
    order = jnp.arange(rows_here, dtype=jnp.int32)
    ahead_mask = (priority[None, :] > priority[:, None]) | (
        priority[None, :] == priority[:, None]
    ) & (order[None, :] < order[:, None])
    target_onehot = target[:, :, None] == jnp.arange(devices_all, dtype=jnp.int32)[None, None, :]
    target_hits = jnp.sum(target_onehot.astype(jnp.bfloat16), axis=1)
    counts = jnp.dot(
        ahead_mask.astype(jnp.bfloat16), target_hits, preferred_element_type=jnp.float32
    )
    position = jnp.sum(
        jnp.where(target_onehot, counts[:, None, :], 0.0), axis=2
    ).astype(jnp.int32)
    granted = jnp.sum(
        jnp.where(target_onehot, capacity.reshape(-1)[None, None, :], 0), axis=2
    )
    accepted = position < granted
    in_plane = (copy_choice * lanes + slot % lanes) * cap_size + position
    code = jnp.where(accepted, (slot // lanes) * plane_slots + in_plane, planes * plane_slots)
    weights_kept = jnp.where(accepted, route_weight, jnp.float32(0.0))
    code_hi = (code // 128).astype(jnp.bfloat16)
    code_lo = (code % 128).astype(jnp.bfloat16)
    w_first = lax.reduce_precision(weights_kept, exponent_bits=8, mantissa_bits=7)
    w_rest = weights_kept - w_first
    w_second = lax.reduce_precision(w_rest, exponent_bits=8, mantissa_bits=7)
    w_third = w_rest - w_second
    meta = jnp.concatenate(
        [code_hi, code_lo]
        + [part.astype(jnp.bfloat16) for part in (w_first, w_second, w_third)],
        axis=1,
    )
    meta_size = rows_here * meta.shape[1]
    meta_rows = -(-meta_size // (8 * features)) * 8
    meta_block = jnp.pad(meta.reshape(-1), (0, meta_rows * features - meta_size))
    packed = jnp.concatenate([normed, meta_block.reshape(meta_rows, features)], axis=0)
    gate_up_local = slot_gate_up[0]
    down_local = slot_down[0]
    hidden_units = down_local.shape[0]
    slot_ids = jnp.arange(plane_slots, dtype=jnp.int32)

    def expert(rows_in):
        gate_up = jnp.dot(rows_in, gate_up_local, preferred_element_type=jnp.float32)
        expert_hidden = (
            jax.nn.silu(gate_up[:, :hidden_units]) * gate_up[:, hidden_units:]
        ).astype(jnp.bfloat16)
        return jnp.dot(expert_hidden, down_local, preferred_element_type=jnp.float32).astype(
            jnp.bfloat16
        )

    received = [packed] + [
        lax.ppermute(packed, "eh", [(i, (i + shift) % planes) for i in range(planes)])
        for shift in range(1, planes)
    ]
    hits = []
    weights_in = []
    buffers = []
    for shift, block in enumerate(received):
        meta_s = (
            block[rows_here:]
            .reshape(-1)[:meta_size]
            .reshape(rows_here, meta.shape[1])
            .astype(jnp.float32)
        )
        code_s = meta_s[:, :picks_row] * 128 + meta_s[:, picks_row : 2 * picks_row]
        local = code_s.astype(jnp.int32) - my_plane * plane_slots
        weights_in.append(
            (meta_s[:, 2 * picks_row : 3 * picks_row] + meta_s[:, 3 * picks_row : 4 * picks_row])
            + meta_s[:, 4 * picks_row :]
        )
        hit = local[None, :, :] == slot_ids[:, None, None]
        hits.append(hit)
        dispatch = jnp.any(hit, axis=2).astype(jnp.bfloat16)
        buffer = jnp.dot(dispatch, block[:rows_here], preferred_element_type=jnp.float32)
        buffers.append(buffer.astype(jnp.bfloat16).reshape(groups * lanes, cap_size, features))
    arrived = lax.all_to_all(
        jnp.stack(buffers, axis=1), PLANE_AXES, split_axis=0, concat_axis=0, tiled=True
    )
    produced = expert(arrived.reshape(-1, features)).reshape(arrived.shape)
    returned_all = lax.all_to_all(produced, PLANE_AXES, split_axis=0, concat_axis=0, tiled=True)
    partials = [None] * planes
    for shift in list(range(1, planes)) + [0]:
        combine = jnp.sum(jnp.where(hits[shift], weights_in[shift][None, :, :], 0.0), axis=2)
        partial = jnp.dot(
            combine.T,
            returned_all[:, shift].reshape(plane_slots, features).astype(jnp.float32),
            precision=lax.Precision.HIGHEST,
            preferred_element_type=jnp.float32,
        )
        if shift:
            back = [((i + shift) % planes, i) for i in range(planes)]
            partial = lax.ppermute(partial.astype(jnp.bfloat16), "eh", back).astype(jnp.float32)
        partials[shift] = partial
    mixture = partials[0]
    for partial in partials[1:]:
        mixture = mixture + partial
    return rms_scale(hidden_state.astype(jnp.float32) + mixture, post_gain).astype(jnp.bfloat16)


def plane_split(devices):
    row = devices[0]
    try:
        coords = [tuple(d.coords) for d in row]
    except AttributeError:
        return 1, len(row)
    best = 0
    for axis in range(len(coords[0])):
        changes = [e for e in range(len(row)) if coords[e][axis] != coords[0][axis]]
        if changes:
            best = max(best, changes[0])
    if best == 0 or len(row) % best or (len(row) // best) % 2:
        return 1, len(row)
    return 2, len(row) // 2


def solution(mesh):
    devices = np.asarray(mesh.devices)
    planes, lanes = plane_split(devices)
    fine = Mesh(devices.reshape(devices.shape[0], planes, lanes), ROWS_AXES)
    rows = P(ROWS_AXES, None)
    placed = (
        rows,
        rows,
        P(None, "grp"),
        P(),
        P(),
        P(SLOT_AXES, None, None),
        P(SLOT_AXES, None, None),
        rows,
        rows,
        P(),
        P(ROWS_AXES),
        P(ROWS_AXES),
        P(),
        rows,
    )
    return jax.shard_map(on_device, mesh=fine, in_specs=placed, out_specs=rows, check_vma=False)
```

```python
import jax
import jax.numpy as jnp
import numpy as np
from jax import lax
from jax.sharding import Mesh
from jax.sharding import PartitionSpec as P

ROWS_AXES = ("grp", "eh", "el")
SLOT_AXES = ("eh", "el")
PLANE_AXES = ("grp", "el")


def rms_scale(values, gain):
    meansq = jnp.mean(values * values, axis=-1, keepdims=True)
    return values * lax.rsqrt(meansq + 1e-06) * gain


def on_device(
    attention,
    residual,
    out_proj,
    pre_gain,
    post_gain,
    slot_gate_up,
    slot_down,
    expert_ids,
    copy_choice,
    placement,
    request_age,
    decode_flag,
    capacity,
    route_weight,
):
    groups = lax.axis_size("grp")
    planes = lax.axis_size("eh")
    lanes = lax.axis_size("el")
    owners = planes * lanes
    devices_all = groups * owners
    rows_here = attention.shape[0]
    features = attention.shape[1]
    picks_row = expert_ids.shape[1]
    cap_size = max(2, rows_here * picks_row // devices_all)
    plane_slots = groups * lanes * cap_size
    my_plane = lax.axis_index("eh")

    me_grp = lax.axis_index("grp")
    blocks = [None] * groups
    blocks[0] = jnp.dot(attention, out_proj, preferred_element_type=jnp.float32)
    for shift in range(1, groups):
        ahead = [(g, (g + shift) % groups) for g in range(groups)]
        back = [(b, a) for a, b in ahead]
        visiting = lax.ppermute(attention, "grp", ahead)
        done = jnp.dot(visiting, out_proj, preferred_element_type=jnp.float32)
        blocks[shift] = lax.ppermute(done, "grp", back)
    order_cols = (jnp.arange(groups, dtype=jnp.int32) - me_grp) % groups
    width = features // groups
    residual_cols = residual.reshape(rows_here, groups, width)
    hidden_blocks = [
        (
            jnp.take(residual_cols, (me_grp + t) % groups, axis=1).astype(jnp.float32)
            + blocks[t]
        ).astype(jnp.bfloat16)
        for t in range(groups)
    ]

    def in_column_order(parts):
        stacked = jnp.stack(parts, axis=0)
        return jnp.concatenate(
            [jnp.take(stacked, order_cols[j], axis=0) for j in range(groups)], axis=1
        )

    hidden_state = in_column_order(hidden_blocks)
    normed = rms_scale(hidden_state.astype(jnp.float32), pre_gain).astype(jnp.bfloat16)
    experts_all = placement.shape[0]
    slot_table = jnp.arange(owners, dtype=jnp.int32)
    matches = (placement[None, :] == jnp.arange(experts_all, dtype=jnp.int32)[:, None]).astype(
        jnp.int32
    )
    slot_of = jnp.sum(slot_table[None, :] * matches, axis=1)
    expert_hits = (
        expert_ids[:, :, None] == jnp.arange(experts_all, dtype=jnp.int32)[None, None, :]
    ).astype(jnp.int32)
    slot = jnp.sum(expert_hits * slot_of[None, None, :], axis=2)
    target = copy_choice * owners + slot
    priority = decode_flag * 1048576 + request_age
    order = jnp.arange(rows_here, dtype=jnp.int32)
    ahead_mask = (priority[None, :] > priority[:, None]) | (
        priority[None, :] == priority[:, None]
    ) & (order[None, :] < order[:, None])
    target_onehot = target[:, :, None] == jnp.arange(devices_all, dtype=jnp.int32)[None, None, :]
    target_hits = jnp.sum(target_onehot.astype(jnp.bfloat16), axis=1)
    counts = jnp.dot(
        ahead_mask.astype(jnp.bfloat16), target_hits, preferred_element_type=jnp.float32
    )
    position = jnp.sum(
        jnp.where(target_onehot, counts[:, None, :], 0.0), axis=2
    ).astype(jnp.int32)
    granted = jnp.sum(
        jnp.where(target_onehot, capacity.reshape(-1)[None, None, :], 0), axis=2
    )
    accepted = position < granted
    in_plane = (copy_choice * lanes + slot % lanes) * cap_size + position
    code = jnp.where(accepted, (slot // lanes) * plane_slots + in_plane, planes * plane_slots)
    weights_kept = jnp.where(accepted, route_weight, jnp.float32(0.0))
    code_hi = (code // 128).astype(jnp.bfloat16)
    code_lo = (code % 128).astype(jnp.bfloat16)
    w_first = lax.reduce_precision(weights_kept, exponent_bits=8, mantissa_bits=7)
    w_rest = weights_kept - w_first
    w_second = lax.reduce_precision(w_rest, exponent_bits=8, mantissa_bits=7)
    w_third = w_rest - w_second
    meta = jnp.concatenate(
        [code_hi, code_lo]
        + [part.astype(jnp.bfloat16) for part in (w_first, w_second, w_third)],
        axis=1,
    )
    meta_size = rows_here * meta.shape[1]
    meta_rows = -(-meta_size // (8 * features)) * 8
    meta_block = jnp.pad(meta.reshape(-1), (0, meta_rows * features - meta_size))
    meta_block = meta_block.reshape(-1, width)
    normed_in = [normed]
    meta_in = [meta_block]
    for shift in range(1, planes):
        ring = [(i, (i + shift) % planes) for i in range(planes)]
        first = lax.ppermute(
            jnp.concatenate([hidden_blocks[0], meta_block], axis=0), "eh", ring
        )
        rest = [first[:rows_here]] + [
            lax.ppermute(hidden_blocks[t], "eh", ring) for t in range(1, groups)
        ]
        meta_in.append(first[rows_here:])
        hidden_s = in_column_order(rest)
        normed_in.append(
            rms_scale(hidden_s.astype(jnp.float32), pre_gain).astype(jnp.bfloat16)
        )
    gate_up_local = slot_gate_up[0]
    down_local = slot_down[0]
    hidden_units = down_local.shape[0]
    slot_ids = jnp.arange(plane_slots, dtype=jnp.int32)

    def expert(rows_in):
        gate_up = jnp.dot(rows_in, gate_up_local, preferred_element_type=jnp.float32)
        expert_hidden = (
            jax.nn.silu(gate_up[:, :hidden_units]) * gate_up[:, hidden_units:]
        ).astype(jnp.bfloat16)
        return jnp.dot(expert_hidden, down_local, preferred_element_type=jnp.float32).astype(
            jnp.bfloat16
        )

    hits = []
    weights_in = []
    buffers = []
    for shift in range(planes):
        meta_s = (
            meta_in[shift]
            .reshape(-1)[:meta_size]
            .reshape(rows_here, meta.shape[1])
            .astype(jnp.float32)
        )
        code_s = meta_s[:, :picks_row] * 128 + meta_s[:, picks_row : 2 * picks_row]
        local = code_s.astype(jnp.int32) - my_plane * plane_slots
        weights_in.append(
            (meta_s[:, 2 * picks_row : 3 * picks_row] + meta_s[:, 3 * picks_row : 4 * picks_row])
            + meta_s[:, 4 * picks_row :]
        )
        hit = local[None, :, :] == slot_ids[:, None, None]
        hits.append(hit)
        dispatch = jnp.any(hit, axis=2).astype(jnp.bfloat16)
        buffer = jnp.dot(dispatch, normed_in[shift], preferred_element_type=jnp.float32)
        buffers.append(buffer.astype(jnp.bfloat16).reshape(groups * lanes, cap_size, features))
    arrived = lax.all_to_all(
        jnp.stack(buffers, axis=1), PLANE_AXES, split_axis=0, concat_axis=0, tiled=True
    )
    produced = expert(arrived.reshape(-1, features)).reshape(arrived.shape)
    returned_all = lax.all_to_all(produced, PLANE_AXES, split_axis=0, concat_axis=0, tiled=True)
    partials = [None] * planes
    for shift in list(range(1, planes)) + [0]:
        combine = jnp.sum(jnp.where(hits[shift], weights_in[shift][None, :, :], 0.0), axis=2)
        partial = jnp.dot(
            combine.T,
            returned_all[:, shift].reshape(plane_slots, features).astype(jnp.float32),
            precision=lax.Precision.HIGHEST,
            preferred_element_type=jnp.float32,
        )
        if shift:
            back = [((i + shift) % planes, i) for i in range(planes)]
            partial = lax.ppermute(partial.astype(jnp.bfloat16), "eh", back).astype(jnp.float32)
        partials[shift] = partial
    mixture = partials[0]
    for partial in partials[1:]:
        mixture = mixture + partial
    return rms_scale(hidden_state.astype(jnp.float32) + mixture, post_gain).astype(jnp.bfloat16)


def plane_split(devices):
    row = devices[0]
    try:
        coords = [tuple(d.coords) for d in row]
    except AttributeError:
        return 1, len(row)
    best = 0
    for axis in range(len(coords[0])):
        changes = [e for e in range(len(row)) if coords[e][axis] != coords[0][axis]]
        if changes:
            best = max(best, changes[0])
    if best == 0 or len(row) % best or (len(row) // best) % 2:
        return 1, len(row)
    return 2, len(row) // 2


def solution(mesh):
    devices = np.asarray(mesh.devices)
    planes, lanes = plane_split(devices)
    fine = Mesh(devices.reshape(devices.shape[0], planes, lanes), ROWS_AXES)
    rows = P(ROWS_AXES, None)
    placed = (
        rows,
        rows,
        P(None, "grp"),
        P(),
        P(),
        P(SLOT_AXES, None, None),
        P(SLOT_AXES, None, None),
        rows,
        rows,
        P(),
        P(ROWS_AXES),
        P(ROWS_AXES),
        P(),
        rows,
    )
    return jax.shard_map(on_device, mesh=fine, in_specs=placed, out_specs=rows, check_vma=False)
```

```python
import jax
import jax.numpy as jnp
import numpy as np
from jax import lax
from jax.sharding import Mesh
from jax.sharding import PartitionSpec as P

ROWS_AXES = ("grp", "eh", "el")
SLOT_AXES = ("eh", "el")
PLANE_AXES = ("grp", "el")


def rms_scale(values, gain):
    meansq = jnp.mean(values * values, axis=-1, keepdims=True)
    return values * lax.rsqrt(meansq + 1e-06) * gain


def on_device(
    attention,
    residual,
    out_proj,
    pre_gain,
    post_gain,
    slot_gate_up,
    slot_down,
    expert_ids,
    copy_choice,
    placement,
    request_age,
    decode_flag,
    capacity,
    route_weight,
):
    groups = lax.axis_size("grp")
    planes = lax.axis_size("eh")
    lanes = lax.axis_size("el")
    owners = planes * lanes
    devices_all = groups * owners
    rows_here = attention.shape[0]
    features = attention.shape[1]
    picks_row = expert_ids.shape[1]
    cap_size = max(2, rows_here * picks_row // devices_all)
    plane_slots = groups * lanes * cap_size
    my_plane = lax.axis_index("eh")

    me_grp = lax.axis_index("grp")
    blocks = [None] * groups
    blocks[0] = jnp.dot(attention, out_proj, preferred_element_type=jnp.float32)
    for shift in range(1, groups):
        ahead = [(g, (g + shift) % groups) for g in range(groups)]
        back = [(b, a) for a, b in ahead]
        visiting = lax.ppermute(attention, "grp", ahead)
        done = jnp.dot(visiting, out_proj, preferred_element_type=jnp.float32)
        blocks[shift] = lax.ppermute(done, "grp", back)
    stacked = jnp.stack(blocks, axis=0)
    order_cols = (jnp.arange(groups, dtype=jnp.int32) - me_grp) % groups
    attn_proj = jnp.concatenate(
        [jnp.take(stacked, order_cols[j], axis=0) for j in range(groups)], axis=1
    )
    hidden_state = (residual.astype(jnp.float32) + attn_proj).astype(jnp.bfloat16)
    normed = rms_scale(hidden_state.astype(jnp.float32), pre_gain).astype(jnp.bfloat16)

    experts_all = placement.shape[0]
    slot_table = jnp.arange(owners, dtype=jnp.int32)
    matches = (placement[None, :] == jnp.arange(experts_all, dtype=jnp.int32)[:, None]).astype(
        jnp.int32
    )
    slot_of = jnp.sum(slot_table[None, :] * matches, axis=1)
    expert_hits = (
        expert_ids[:, :, None] == jnp.arange(experts_all, dtype=jnp.int32)[None, None, :]
    ).astype(jnp.int32)
    slot = jnp.sum(expert_hits * slot_of[None, None, :], axis=2)
    target = copy_choice * owners + slot
    priority = decode_flag * 1048576 + request_age
    order = jnp.arange(rows_here, dtype=jnp.int32)
    ahead_mask = (priority[None, :] > priority[:, None]) | (
        priority[None, :] == priority[:, None]
    ) & (order[None, :] < order[:, None])
    target_onehot = target[:, :, None] == jnp.arange(devices_all, dtype=jnp.int32)[None, None, :]
    target_hits = jnp.sum(target_onehot.astype(jnp.bfloat16), axis=1)
    counts = jnp.dot(
        ahead_mask.astype(jnp.bfloat16), target_hits, preferred_element_type=jnp.float32
    )
    position = jnp.sum(
        jnp.where(target_onehot, counts[:, None, :], 0.0), axis=2
    ).astype(jnp.int32)
    granted = jnp.sum(
        jnp.where(target_onehot, capacity.reshape(-1)[None, None, :], 0), axis=2
    )
    accepted = position < granted
    in_plane = (copy_choice * lanes + slot % lanes) * cap_size + position
    code = jnp.where(accepted, (slot // lanes) * plane_slots + in_plane, planes * plane_slots)
    weights_kept = jnp.where(accepted, route_weight, jnp.float32(0.0))
    code_hi = (code // 128).astype(jnp.bfloat16)
    code_lo = (code % 128).astype(jnp.bfloat16)
    w_first = lax.reduce_precision(weights_kept, exponent_bits=8, mantissa_bits=7)
    w_rest = weights_kept - w_first
    w_second = lax.reduce_precision(w_rest, exponent_bits=8, mantissa_bits=7)
    w_third = w_rest - w_second
    meta = jnp.concatenate(
        [code_hi, code_lo]
        + [part.astype(jnp.bfloat16) for part in (w_first, w_second, w_third)],
        axis=1,
    )
    meta_size = rows_here * meta.shape[1]
    meta_rows = -(-meta_size // (8 * features)) * 8
    meta_block = jnp.pad(meta.reshape(-1), (0, meta_rows * features - meta_size))
    packed = jnp.concatenate([normed, meta_block.reshape(meta_rows, features)], axis=0)
    gate_up_local = slot_gate_up[0]
    down_local = slot_down[0]
    hidden_units = down_local.shape[0]
    slot_ids = jnp.arange(plane_slots, dtype=jnp.int32)

    def expert(rows_in):
        gate_up = jnp.dot(rows_in, gate_up_local, preferred_element_type=jnp.float32)
        expert_hidden = (
            jax.nn.silu(gate_up[:, :hidden_units]) * gate_up[:, hidden_units:]
        ).astype(jnp.bfloat16)
        return jnp.dot(expert_hidden, down_local, preferred_element_type=jnp.float32).astype(
            jnp.bfloat16
        )

    gathered = lax.all_gather(packed, "eh", axis=0)
    received = [packed] + [
        jnp.take(gathered, (my_plane - shift) % planes, axis=0) for shift in range(1, planes)
    ]
    hits = []
    weights_in = []
    buffers = []
    for shift, block in enumerate(received):
        meta_s = (
            block[rows_here:]
            .reshape(-1)[:meta_size]
            .reshape(rows_here, meta.shape[1])
            .astype(jnp.float32)
        )
        code_s = meta_s[:, :picks_row] * 128 + meta_s[:, picks_row : 2 * picks_row]
        local = code_s.astype(jnp.int32) - my_plane * plane_slots
        weights_in.append(
            (meta_s[:, 2 * picks_row : 3 * picks_row] + meta_s[:, 3 * picks_row : 4 * picks_row])
            + meta_s[:, 4 * picks_row :]
        )
        hit = local[None, :, :] == slot_ids[:, None, None]
        hits.append(hit)
        dispatch = jnp.any(hit, axis=2).astype(jnp.bfloat16)
        buffer = jnp.dot(dispatch, block[:rows_here], preferred_element_type=jnp.float32)
        buffers.append(buffer.astype(jnp.bfloat16).reshape(groups * lanes, cap_size, features))
    arrived = lax.all_to_all(
        jnp.stack(buffers, axis=1), PLANE_AXES, split_axis=0, concat_axis=0, tiled=True
    )
    produced = expert(arrived.reshape(-1, features)).reshape(arrived.shape)
    returned_all = lax.all_to_all(produced, PLANE_AXES, split_axis=0, concat_axis=0, tiled=True)
    partials = [None] * planes
    for shift in list(range(1, planes)) + [0]:
        combine = jnp.sum(jnp.where(hits[shift], weights_in[shift][None, :, :], 0.0), axis=2)
        partial = jnp.dot(
            combine.T,
            returned_all[:, shift].reshape(plane_slots, features).astype(jnp.float32),
            precision=lax.Precision.HIGHEST,
            preferred_element_type=jnp.float32,
        )
        if shift:
            back = [((i + shift) % planes, i) for i in range(planes)]
            partial = lax.ppermute(partial.astype(jnp.bfloat16), "eh", back).astype(jnp.float32)
        partials[shift] = partial
    mixture = partials[0]
    for partial in partials[1:]:
        mixture = mixture + partial
    return rms_scale(hidden_state.astype(jnp.float32) + mixture, post_gain).astype(jnp.bfloat16)


def plane_split(devices):
    row = devices[0]
    try:
        coords = [tuple(d.coords) for d in row]
    except AttributeError:
        return 1, len(row)
    best = 0
    for axis in range(len(coords[0])):
        changes = [e for e in range(len(row)) if coords[e][axis] != coords[0][axis]]
        if changes:
            best = max(best, changes[0])
    if best == 0 or len(row) % best or (len(row) // best) % 2:
        return 1, len(row)
    return 2, len(row) // 2


def solution(mesh):
    devices = np.asarray(mesh.devices)
    planes, lanes = plane_split(devices)
    fine = Mesh(devices.reshape(devices.shape[0], planes, lanes), ROWS_AXES)
    rows = P(ROWS_AXES, None)
    placed = (
        rows,
        rows,
        P(None, "grp"),
        P(),
        P(),
        P(SLOT_AXES, None, None),
        P(SLOT_AXES, None, None),
        rows,
        rows,
        P(),
        P(ROWS_AXES),
        P(ROWS_AXES),
        P(),
        rows,
    )
    return jax.shard_map(on_device, mesh=fine, in_specs=placed, out_specs=rows, check_vma=False)
```

```python
import jax
import jax.numpy as jnp
import numpy as np
from jax import lax
from jax.sharding import Mesh
from jax.sharding import PartitionSpec as P

ROWS_AXES = ("grp", "eh", "el")
SLOT_AXES = ("eh", "el")
PLANE_AXES = ("grp", "el")


def rms_scale(values, gain):
    meansq = jnp.mean(values * values, axis=-1, keepdims=True)
    return values * lax.rsqrt(meansq + 1e-06) * gain


def on_device(
    attention,
    residual,
    out_proj,
    pre_gain,
    post_gain,
    slot_gate_up,
    slot_down,
    expert_ids,
    copy_choice,
    placement,
    request_age,
    decode_flag,
    capacity,
    route_weight,
):
    groups = lax.axis_size("grp")
    planes = lax.axis_size("eh")
    lanes = lax.axis_size("el")
    owners = planes * lanes
    devices_all = groups * owners
    rows_here = attention.shape[0]
    features = attention.shape[1]
    picks_row = expert_ids.shape[1]
    cap_size = max(2, rows_here * picks_row // devices_all)
    plane_slots = groups * lanes * cap_size
    my_plane = lax.axis_index("eh")

    me_grp = lax.axis_index("grp")
    blocks = [None] * groups
    blocks[0] = jnp.dot(attention, out_proj, preferred_element_type=jnp.float32)
    for shift in range(1, groups):
        ahead = [(g, (g + shift) % groups) for g in range(groups)]
        back = [(b, a) for a, b in ahead]
        visiting = lax.ppermute(attention, "grp", ahead)
        done = jnp.dot(visiting, out_proj, preferred_element_type=jnp.float32)
        blocks[shift] = lax.ppermute(done, "grp", back)
    stacked = jnp.stack(blocks, axis=0)
    order_cols = (jnp.arange(groups, dtype=jnp.int32) - me_grp) % groups
    attn_proj = jnp.concatenate(
        [jnp.take(stacked, order_cols[j], axis=0) for j in range(groups)], axis=1
    )
    hidden_state = (residual.astype(jnp.float32) + attn_proj).astype(jnp.bfloat16)
    normed = rms_scale(hidden_state.astype(jnp.float32), pre_gain).astype(jnp.bfloat16)

    experts_all = placement.shape[0]
    slot_table = jnp.arange(owners, dtype=jnp.int32)
    matches = (placement[None, :] == jnp.arange(experts_all, dtype=jnp.int32)[:, None]).astype(
        jnp.int32
    )
    slot_of = jnp.sum(slot_table[None, :] * matches, axis=1)
    expert_hits = (
        expert_ids[:, :, None] == jnp.arange(experts_all, dtype=jnp.int32)[None, None, :]
    ).astype(jnp.int32)
    slot = jnp.sum(expert_hits * slot_of[None, None, :], axis=2)
    target = copy_choice * owners + slot
    priority = decode_flag * 1048576 + request_age
    order = jnp.arange(rows_here, dtype=jnp.int32)
    ahead_mask = (priority[None, :] > priority[:, None]) | (
        priority[None, :] == priority[:, None]
    ) & (order[None, :] < order[:, None])
    target_onehot = target[:, :, None] == jnp.arange(devices_all, dtype=jnp.int32)[None, None, :]
    target_hits = jnp.sum(target_onehot.astype(jnp.bfloat16), axis=1)
    counts = jnp.dot(
        ahead_mask.astype(jnp.bfloat16), target_hits, preferred_element_type=jnp.float32
    )
    position = jnp.sum(
        jnp.where(target_onehot, counts[:, None, :], 0.0), axis=2
    ).astype(jnp.int32)
    granted = jnp.sum(
        jnp.where(target_onehot, capacity.reshape(-1)[None, None, :], 0), axis=2
    )
    accepted = position < granted
    in_plane = (copy_choice * lanes + slot % lanes) * cap_size + position
    code = jnp.where(accepted, (slot // lanes) * plane_slots + in_plane, planes * plane_slots)
    weights_kept = jnp.where(accepted, route_weight, jnp.float32(0.0))
    code_hi = (code // 128).astype(jnp.bfloat16)
    code_lo = (code % 128).astype(jnp.bfloat16)
    w_first = lax.reduce_precision(weights_kept, exponent_bits=8, mantissa_bits=7)
    w_rest = weights_kept - w_first
    w_second = lax.reduce_precision(w_rest, exponent_bits=8, mantissa_bits=7)
    w_third = w_rest - w_second
    meta = jnp.concatenate(
        [code_hi, code_lo]
        + [part.astype(jnp.bfloat16) for part in (w_first, w_second, w_third)],
        axis=1,
    )
    meta_size = rows_here * meta.shape[1]
    meta_rows = -(-meta_size // (8 * features)) * 8
    meta_block = jnp.pad(meta.reshape(-1), (0, meta_rows * features - meta_size))
    packed = jnp.concatenate([normed, meta_block.reshape(meta_rows, features)], axis=0)
    gate_up_local = slot_gate_up[0]
    down_local = slot_down[0]
    hidden_units = down_local.shape[0]
    slot_ids = jnp.arange(plane_slots, dtype=jnp.int32)

    def expert(rows_in):
        gate_up = jnp.dot(rows_in, gate_up_local, preferred_element_type=jnp.float32)
        expert_hidden = (
            jax.nn.silu(gate_up[:, :hidden_units]) * gate_up[:, hidden_units:]
        ).astype(jnp.bfloat16)
        return jnp.dot(expert_hidden, down_local, preferred_element_type=jnp.float32).astype(
            jnp.bfloat16
        )

    received = [packed] + [
        lax.ppermute(packed, "eh", [(i, (i + shift) % planes) for i in range(planes)])
        for shift in range(1, planes)
    ]
    hits = []
    weights_in = []
    buffers = []
    for shift, block in enumerate(received):
        meta_s = (
            block[rows_here:]
            .reshape(-1)[:meta_size]
            .reshape(rows_here, meta.shape[1])
            .astype(jnp.float32)
        )
        code_s = meta_s[:, :picks_row] * 128 + meta_s[:, picks_row : 2 * picks_row]
        local = code_s.astype(jnp.int32) - my_plane * plane_slots
        weights_in.append(
            (meta_s[:, 2 * picks_row : 3 * picks_row] + meta_s[:, 3 * picks_row : 4 * picks_row])
            + meta_s[:, 4 * picks_row :]
        )
        hit = local[None, :, :] == slot_ids[:, None, None]
        hits.append(hit)
        dispatch = jnp.any(hit, axis=2).astype(jnp.bfloat16)
        buffer = jnp.dot(dispatch, block[:rows_here], preferred_element_type=jnp.float32)
        buffers.append(buffer.astype(jnp.bfloat16).reshape(groups * lanes, cap_size, features))
    arrived = lax.all_to_all(
        jnp.stack(buffers, axis=1), PLANE_AXES, split_axis=0, concat_axis=0, tiled=True
    )
    produced = expert(arrived.reshape(-1, features)).reshape(arrived.shape)
    partials = [None] * planes
    for shift in list(range(1, planes)) + [0]:
        returned = lax.all_to_all(
            produced[:, shift], PLANE_AXES, split_axis=0, concat_axis=0, tiled=True
        )
        combine = jnp.sum(jnp.where(hits[shift], weights_in[shift][None, :, :], 0.0), axis=2)
        partial = jnp.dot(
            combine.T,
            returned.reshape(plane_slots, features).astype(jnp.float32),
            precision=lax.Precision.HIGHEST,
            preferred_element_type=jnp.float32,
        )
        if shift:
            back = [((i + shift) % planes, i) for i in range(planes)]
            partial = lax.ppermute(partial.astype(jnp.bfloat16), "eh", back).astype(jnp.float32)
        partials[shift] = partial
    mixture = partials[0]
    for partial in partials[1:]:
        mixture = mixture + partial
    return rms_scale(hidden_state.astype(jnp.float32) + mixture, post_gain).astype(jnp.bfloat16)


def plane_split(devices):
    row = devices[0]
    try:
        coords = [tuple(d.coords) for d in row]
    except AttributeError:
        return 1, len(row)
    best = 0
    for axis in range(len(coords[0])):
        changes = [e for e in range(len(row)) if coords[e][axis] != coords[0][axis]]
        if changes:
            best = max(best, changes[0])
    if best == 0 or len(row) % best or (len(row) // best) % 2:
        return 1, len(row)
    return 2, len(row) // 2


def solution(mesh):
    devices = np.asarray(mesh.devices)
    planes, lanes = plane_split(devices)
    fine = Mesh(devices.reshape(devices.shape[0], planes, lanes), ROWS_AXES)
    rows = P(ROWS_AXES, None)
    placed = (
        rows,
        rows,
        P(None, "grp"),
        P(),
        P(),
        P(SLOT_AXES, None, None),
        P(SLOT_AXES, None, None),
        rows,
        rows,
        P(),
        P(ROWS_AXES),
        P(ROWS_AXES),
        P(),
        rows,
    )
    return jax.shard_map(on_device, mesh=fine, in_specs=placed, out_specs=rows, check_vma=False)
```

```python
import jax
import jax.numpy as jnp
import numpy as np
from jax import lax
from jax.sharding import Mesh
from jax.sharding import PartitionSpec as P

ROWS_AXES = ("grp", "eh", "el")
SLOT_AXES = ("eh", "el")
PLANE_AXES = ("grp", "el")


def rms_scale(values, gain):
    meansq = jnp.mean(values * values, axis=-1, keepdims=True)
    return values * lax.rsqrt(meansq + 1e-06) * gain


def on_device(
    attention,
    residual,
    out_proj,
    pre_gain,
    post_gain,
    slot_gate_up,
    slot_down,
    expert_ids,
    copy_choice,
    placement,
    request_age,
    decode_flag,
    capacity,
    route_weight,
):
    groups = lax.axis_size("grp")
    planes = lax.axis_size("eh")
    lanes = lax.axis_size("el")
    owners = planes * lanes
    devices_all = groups * owners
    rows_here = attention.shape[0]
    features = attention.shape[1]
    picks_row = expert_ids.shape[1]
    cap_size = max(2, rows_here * picks_row // devices_all)
    plane_slots = groups * lanes * cap_size
    my_plane = lax.axis_index("eh")

    me_grp = lax.axis_index("grp")
    blocks = [None] * groups
    blocks[0] = jnp.dot(attention, out_proj, preferred_element_type=jnp.float32)
    for shift in range(1, groups):
        ahead = [(g, (g + shift) % groups) for g in range(groups)]
        back = [(b, a) for a, b in ahead]
        visiting = lax.ppermute(attention, "grp", ahead)
        done = jnp.dot(visiting, out_proj, preferred_element_type=jnp.float32)
        blocks[shift] = lax.ppermute(done, "grp", back)
    stacked = jnp.stack(blocks, axis=0)
    order_cols = (jnp.arange(groups, dtype=jnp.int32) - me_grp) % groups
    attn_proj = jnp.concatenate(
        [jnp.take(stacked, order_cols[j], axis=0) for j in range(groups)], axis=1
    )
    hidden_state = (residual.astype(jnp.float32) + attn_proj).astype(jnp.bfloat16)
    normed = rms_scale(hidden_state.astype(jnp.float32), pre_gain).astype(jnp.bfloat16)

    experts_all = placement.shape[0]
    slot_table = jnp.arange(owners, dtype=jnp.int32)
    matches = (placement[None, :] == jnp.arange(experts_all, dtype=jnp.int32)[:, None]).astype(
        jnp.int32
    )
    slot_of = jnp.sum(slot_table[None, :] * matches, axis=1)
    expert_hits = (
        expert_ids[:, :, None] == jnp.arange(experts_all, dtype=jnp.int32)[None, None, :]
    ).astype(jnp.int32)
    slot = jnp.sum(expert_hits * slot_of[None, None, :], axis=2)
    target = copy_choice * owners + slot
    priority = decode_flag * 1048576 + request_age
    order = jnp.arange(rows_here, dtype=jnp.int32)
    ahead_mask = (priority[None, :] > priority[:, None]) | (
        priority[None, :] == priority[:, None]
    ) & (order[None, :] < order[:, None])
    target_onehot = target[:, :, None] == jnp.arange(devices_all, dtype=jnp.int32)[None, None, :]
    target_hits = jnp.sum(target_onehot.astype(jnp.bfloat16), axis=1)
    counts = jnp.dot(
        ahead_mask.astype(jnp.bfloat16), target_hits, preferred_element_type=jnp.float32
    )
    position = jnp.sum(
        jnp.where(target_onehot, counts[:, None, :], 0.0), axis=2
    ).astype(jnp.int32)
    granted = jnp.sum(
        jnp.where(target_onehot, capacity.reshape(-1)[None, None, :], 0), axis=2
    )
    accepted = position < granted
    in_plane = (copy_choice * lanes + slot % lanes) * cap_size + position
    code = jnp.where(accepted, (slot // lanes) * plane_slots + in_plane, planes * plane_slots)
    weights_kept = jnp.where(accepted, route_weight, jnp.float32(0.0))
    code_hi = (code // 128).astype(jnp.bfloat16)
    code_lo = (code % 128).astype(jnp.bfloat16)
    w_first = lax.reduce_precision(weights_kept, exponent_bits=8, mantissa_bits=7)
    w_rest = weights_kept - w_first
    w_second = lax.reduce_precision(w_rest, exponent_bits=8, mantissa_bits=7)
    w_third = w_rest - w_second
    meta = jnp.concatenate(
        [code_hi, code_lo]
        + [part.astype(jnp.bfloat16) for part in (w_first, w_second, w_third)],
        axis=1,
    )
    meta_size = rows_here * meta.shape[1]
    meta_rows = -(-meta_size // (8 * features)) * 8
    meta_block = jnp.pad(meta.reshape(-1), (0, meta_rows * features - meta_size))
    packed = jnp.concatenate([normed, meta_block.reshape(meta_rows, features)], axis=0)
    gate_up_local = slot_gate_up[0]
    down_local = slot_down[0]
    hidden_units = down_local.shape[0]
    slot_ids = jnp.arange(plane_slots, dtype=jnp.int32)

    def expert(rows_in):
        gate_up = jnp.dot(rows_in, gate_up_local, preferred_element_type=jnp.float32)
        expert_hidden = (
            jax.nn.silu(gate_up[:, :hidden_units]) * gate_up[:, hidden_units:]
        ).astype(jnp.bfloat16)
        return jnp.dot(expert_hidden, down_local, preferred_element_type=jnp.float32).astype(
            jnp.bfloat16
        )

    received = [packed] + [
        lax.ppermute(packed, "eh", [(i, (i + shift) % planes) for i in range(planes)])
        for shift in range(1, planes)
    ]
    hits = []
    weights_in = []
    buffers = []
    for shift, block in enumerate(received):
        meta_s = (
            block[rows_here:]
            .reshape(-1)[:meta_size]
            .reshape(rows_here, meta.shape[1])
            .astype(jnp.float32)
        )
        code_s = meta_s[:, :picks_row] * 128 + meta_s[:, picks_row : 2 * picks_row]
        local = code_s.astype(jnp.int32) - my_plane * plane_slots
        weights_in.append(
            (meta_s[:, 2 * picks_row : 3 * picks_row] + meta_s[:, 3 * picks_row : 4 * picks_row])
            + meta_s[:, 4 * picks_row :]
        )
        hit = local[None, :, :] == slot_ids[:, None, None]
        hits.append(hit)
        dispatch = jnp.any(hit, axis=2).astype(jnp.bfloat16)
        buffer = jnp.dot(dispatch, block[:rows_here], preferred_element_type=jnp.float32)
        buffers.append(buffer.astype(jnp.bfloat16).reshape(groups * lanes, cap_size, features))
    arrived = lax.all_to_all(
        jnp.stack(buffers, axis=0), PLANE_AXES, split_axis=1, concat_axis=1, tiled=True
    )
    produced = expert(arrived.reshape(-1, features)).reshape(arrived.shape)
    partials = [None] * planes
    for shift in list(range(1, planes)) + [0]:
        returned = lax.all_to_all(
            produced[shift], PLANE_AXES, split_axis=0, concat_axis=0, tiled=True
        )
        combine = jnp.sum(jnp.where(hits[shift], weights_in[shift][None, :, :], 0.0), axis=2)
        partial = jnp.dot(
            combine.T,
            returned.reshape(plane_slots, features).astype(jnp.float32),
            precision=lax.Precision.HIGHEST,
            preferred_element_type=jnp.float32,
        )
        if shift:
            back = [((i + shift) % planes, i) for i in range(planes)]
            partial = lax.ppermute(partial.astype(jnp.bfloat16), "eh", back).astype(jnp.float32)
        partials[shift] = partial
    mixture = partials[0]
    for partial in partials[1:]:
        mixture = mixture + partial
    return rms_scale(hidden_state.astype(jnp.float32) + mixture, post_gain).astype(jnp.bfloat16)


def plane_split(devices):
    row = devices[0]
    try:
        coords = [tuple(d.coords) for d in row]
    except AttributeError:
        return 1, len(row)
    best = 0
    for axis in range(len(coords[0])):
        changes = [e for e in range(len(row)) if coords[e][axis] != coords[0][axis]]
        if changes:
            best = max(best, changes[0])
    if best == 0 or len(row) % best or (len(row) // best) % 2:
        return 1, len(row)
    return 2, len(row) // 2


def solution(mesh):
    devices = np.asarray(mesh.devices)
    planes, lanes = plane_split(devices)
    fine = Mesh(devices.reshape(devices.shape[0], planes, lanes), ROWS_AXES)
    rows = P(ROWS_AXES, None)
    placed = (
        rows,
        rows,
        P(None, "grp"),
        P(),
        P(),
        P(SLOT_AXES, None, None),
        P(SLOT_AXES, None, None),
        rows,
        rows,
        P(),
        P(ROWS_AXES),
        P(ROWS_AXES),
        P(),
        rows,
    )
    return jax.shard_map(on_device, mesh=fine, in_specs=placed, out_specs=rows, check_vma=False)
```

```python
import jax
import jax.numpy as jnp
import numpy as np
from jax import lax
from jax.sharding import Mesh
from jax.sharding import PartitionSpec as P

ROWS_AXES = ("grp", "eh", "el")
SLOT_AXES = ("eh", "el")
PLANE_AXES = ("grp", "el")


def rms_scale(values, gain):
    meansq = jnp.mean(values * values, axis=-1, keepdims=True)
    return values * lax.rsqrt(meansq + 1e-06) * gain


def on_device(
    attention,
    residual,
    out_proj,
    pre_gain,
    post_gain,
    slot_gate_up,
    slot_down,
    expert_ids,
    copy_choice,
    placement,
    request_age,
    decode_flag,
    capacity,
    route_weight,
):
    groups = lax.axis_size("grp")
    planes = lax.axis_size("eh")
    lanes = lax.axis_size("el")
    owners = planes * lanes
    devices_all = groups * owners
    rows_here = attention.shape[0]
    features = attention.shape[1]
    picks_row = expert_ids.shape[1]
    cap_size = max(2, rows_here * picks_row // devices_all)
    plane_slots = groups * lanes * cap_size
    my_plane = lax.axis_index("eh")

    me_grp = lax.axis_index("grp")
    blocks = [None] * groups
    blocks[0] = jnp.dot(attention, out_proj, preferred_element_type=jnp.float32)
    for shift in range(1, groups):
        ahead = [(g, (g + shift) % groups) for g in range(groups)]
        back = [(b, a) for a, b in ahead]
        visiting = lax.ppermute(attention, "grp", ahead)
        done = jnp.dot(visiting, out_proj, preferred_element_type=jnp.float32)
        blocks[shift] = lax.ppermute(done, "grp", back)
    stacked = jnp.stack(blocks, axis=0)
    order_cols = (jnp.arange(groups, dtype=jnp.int32) - me_grp) % groups
    attn_proj = jnp.concatenate(
        [jnp.take(stacked, order_cols[j], axis=0) for j in range(groups)], axis=1
    )
    hidden_state = (residual.astype(jnp.float32) + attn_proj).astype(jnp.bfloat16)
    normed = rms_scale(hidden_state.astype(jnp.float32), pre_gain).astype(jnp.bfloat16)

    experts_all = placement.shape[0]
    slot_table = jnp.arange(owners, dtype=jnp.int32)
    matches = (placement[None, :] == jnp.arange(experts_all, dtype=jnp.int32)[:, None]).astype(
        jnp.int32
    )
    slot_of = jnp.sum(slot_table[None, :] * matches, axis=1)
    expert_hits = (
        expert_ids[:, :, None] == jnp.arange(experts_all, dtype=jnp.int32)[None, None, :]
    ).astype(jnp.int32)
    slot = jnp.sum(expert_hits * slot_of[None, None, :], axis=2)
    target = copy_choice * owners + slot
    priority = decode_flag * 1048576 + request_age
    order = jnp.arange(rows_here, dtype=jnp.int32)
    ahead_mask = (priority[None, :] > priority[:, None]) | (
        priority[None, :] == priority[:, None]
    ) & (order[None, :] < order[:, None])
    target_onehot = target[:, :, None] == jnp.arange(devices_all, dtype=jnp.int32)[None, None, :]
    target_hits = jnp.sum(target_onehot.astype(jnp.bfloat16), axis=1)
    counts = jnp.dot(
        ahead_mask.astype(jnp.bfloat16), target_hits, preferred_element_type=jnp.float32
    )
    position = jnp.sum(
        jnp.where(target_onehot, counts[:, None, :], 0.0), axis=2
    ).astype(jnp.int32)
    granted = jnp.sum(
        jnp.where(target_onehot, capacity.reshape(-1)[None, None, :], 0), axis=2
    )
    accepted = position < granted
    in_plane = (copy_choice * lanes + slot % lanes) * cap_size + position
    code = jnp.where(accepted, (slot // lanes) * plane_slots + in_plane, planes * plane_slots)
    weights_kept = jnp.where(accepted, route_weight, jnp.float32(0.0))
    code_hi = (code // 128).astype(jnp.bfloat16)
    code_lo = (code % 128).astype(jnp.bfloat16)
    w_first = lax.reduce_precision(weights_kept, exponent_bits=8, mantissa_bits=7)
    w_rest = weights_kept - w_first
    w_second = lax.reduce_precision(w_rest, exponent_bits=8, mantissa_bits=7)
    w_third = w_rest - w_second
    meta = jnp.concatenate(
        [code_hi, code_lo]
        + [part.astype(jnp.bfloat16) for part in (w_first, w_second, w_third)],
        axis=1,
    )
    meta_size = rows_here * meta.shape[1]
    meta_rows = -(-meta_size // (8 * features)) * 8
    meta_block = jnp.pad(meta.reshape(-1), (0, meta_rows * features - meta_size))
    packed = jnp.concatenate([normed, meta_block.reshape(meta_rows, features)], axis=0)
    gate_up_local = slot_gate_up[0]
    down_local = slot_down[0]
    hidden_units = down_local.shape[0]
    slot_ids = jnp.arange(plane_slots, dtype=jnp.int32)

    def expert(rows_in):
        gate_up = jnp.dot(rows_in, gate_up_local, preferred_element_type=jnp.float32)
        expert_hidden = (
            jax.nn.silu(gate_up[:, :hidden_units]) * gate_up[:, hidden_units:]
        ).astype(jnp.bfloat16)
        return jnp.dot(expert_hidden, down_local, preferred_element_type=jnp.float32).astype(
            jnp.bfloat16
        )

    received = [packed] + [
        lax.ppermute(packed, "eh", [(i, (i + shift) % planes) for i in range(planes)])
        for shift in range(1, planes)
    ]
    hits = []
    weights_in = []
    buffers = []
    for shift, block in enumerate(received):
        meta_s = (
            block[rows_here:]
            .reshape(-1)[:meta_size]
            .reshape(rows_here, meta.shape[1])
            .astype(jnp.float32)
        )
        code_s = meta_s[:, :picks_row] * 128 + meta_s[:, picks_row : 2 * picks_row]
        local = code_s.astype(jnp.int32) - my_plane * plane_slots
        weights_in.append(
            (meta_s[:, 2 * picks_row : 3 * picks_row] + meta_s[:, 3 * picks_row : 4 * picks_row])
            + meta_s[:, 4 * picks_row :]
        )
        hit = local[None, :, :] == slot_ids[:, None, None]
        hits.append(hit)
        dispatch = jnp.any(hit, axis=2).astype(jnp.bfloat16)
        buffer = jnp.dot(dispatch, block[:rows_here], preferred_element_type=jnp.float32)
        buffers.append(buffer.astype(jnp.bfloat16).reshape(groups * lanes, cap_size, features))
    arrived = lax.all_to_all(
        jnp.stack(buffers, axis=1), PLANE_AXES, split_axis=0, concat_axis=0, tiled=True
    )
    produced = expert(arrived.reshape(-1, features)).reshape(arrived.shape)
    partials = [None] * planes
    for shift in list(range(1, planes)) + [0]:
        returned = lax.all_to_all(
            produced[:, shift], PLANE_AXES, split_axis=0, concat_axis=0, tiled=True
        )
        combine = jnp.sum(jnp.where(hits[shift], weights_in[shift][None, :, :], 0.0), axis=2)
        partial = jnp.dot(
            combine.T,
            returned.reshape(plane_slots, features).astype(jnp.float32),
            precision=lax.Precision.HIGH,
            preferred_element_type=jnp.float32,
        )
        if shift:
            back = [((i + shift) % planes, i) for i in range(planes)]
            partial = lax.ppermute(partial.astype(jnp.bfloat16), "eh", back).astype(jnp.float32)
        partials[shift] = partial
    mixture = partials[0]
    for partial in partials[1:]:
        mixture = mixture + partial
    return rms_scale(hidden_state.astype(jnp.float32) + mixture, post_gain).astype(jnp.bfloat16)


def plane_split(devices):
    row = devices[0]
    try:
        coords = [tuple(d.coords) for d in row]
    except AttributeError:
        return 1, len(row)
    best = 0
    for axis in range(len(coords[0])):
        changes = [e for e in range(len(row)) if coords[e][axis] != coords[0][axis]]
        if changes:
            best = max(best, changes[0])
    if best == 0 or len(row) % best or (len(row) // best) % 2:
        return 1, len(row)
    return 2, len(row) // 2


def solution(mesh):
    devices = np.asarray(mesh.devices)
    planes, lanes = plane_split(devices)
    fine = Mesh(devices.reshape(devices.shape[0], planes, lanes), ROWS_AXES)
    rows = P(ROWS_AXES, None)
    placed = (
        rows,
        rows,
        P(None, "grp"),
        P(),
        P(),
        P(SLOT_AXES, None, None),
        P(SLOT_AXES, None, None),
        rows,
        rows,
        P(),
        P(ROWS_AXES),
        P(ROWS_AXES),
        P(),
        rows,
    )
    return jax.shard_map(on_device, mesh=fine, in_specs=placed, out_specs=rows, check_vma=False)
```

```python
import jax
import jax.numpy as jnp
import numpy as np
from jax import lax
from jax.sharding import Mesh
from jax.sharding import PartitionSpec as P

ROWS_AXES = ("grp", "eh", "el")
SLOT_AXES = ("eh", "el")
PLANE_AXES = ("grp", "el")


def rms_scale(values, gain):
    meansq = jnp.mean(values * values, axis=-1, keepdims=True)
    return values * lax.rsqrt(meansq + 1e-06) * gain


def on_device(
    attention,
    residual,
    out_proj,
    pre_gain,
    post_gain,
    slot_gate_up,
    slot_down,
    expert_ids,
    copy_choice,
    placement,
    request_age,
    decode_flag,
    capacity,
    route_weight,
):
    groups = lax.axis_size("grp")
    planes = lax.axis_size("eh")
    lanes = lax.axis_size("el")
    owners = planes * lanes
    devices_all = groups * owners
    rows_here = attention.shape[0]
    features = attention.shape[1]
    picks_row = expert_ids.shape[1]
    cap_size = max(2, rows_here * picks_row // devices_all)
    plane_slots = groups * lanes * cap_size
    my_plane = lax.axis_index("eh")

    me_grp = lax.axis_index("grp")
    width = features // groups
    residual_cols = residual.reshape(rows_here, groups, width)
    hidden_blocks = [
        (
            jnp.take(residual_cols, me_grp, axis=1).astype(jnp.float32)
            + jnp.dot(attention, out_proj, preferred_element_type=jnp.float32)
        ).astype(jnp.bfloat16)
    ]
    for shift in range(1, groups):
        ahead = [(g, (g + shift) % groups) for g in range(groups)]
        back = [(b, a) for a, b in ahead]
        payload = jnp.concatenate(
            [attention, jnp.take(residual_cols, (me_grp + shift) % groups, axis=1)], axis=1
        )
        visiting = lax.ppermute(payload, "grp", ahead)
        done = (
            visiting[:, features:].astype(jnp.float32)
            + jnp.dot(visiting[:, :features], out_proj, preferred_element_type=jnp.float32)
        ).astype(jnp.bfloat16)
        hidden_blocks.append(lax.ppermute(done, "grp", back))
    order_cols = (jnp.arange(groups, dtype=jnp.int32) - me_grp) % groups
    stacked = jnp.stack(hidden_blocks, axis=0)
    hidden_state = jnp.concatenate(
        [jnp.take(stacked, order_cols[j], axis=0) for j in range(groups)], axis=1
    )
    normed = rms_scale(hidden_state.astype(jnp.float32), pre_gain).astype(jnp.bfloat16)

    experts_all = placement.shape[0]
    slot_table = jnp.arange(owners, dtype=jnp.int32)
    matches = (placement[None, :] == jnp.arange(experts_all, dtype=jnp.int32)[:, None]).astype(
        jnp.int32
    )
    slot_of = jnp.sum(slot_table[None, :] * matches, axis=1)
    expert_hits = (
        expert_ids[:, :, None] == jnp.arange(experts_all, dtype=jnp.int32)[None, None, :]
    ).astype(jnp.int32)
    slot = jnp.sum(expert_hits * slot_of[None, None, :], axis=2)
    target = copy_choice * owners + slot
    priority = decode_flag * 1048576 + request_age
    order = jnp.arange(rows_here, dtype=jnp.int32)
    ahead_mask = (priority[None, :] > priority[:, None]) | (
        priority[None, :] == priority[:, None]
    ) & (order[None, :] < order[:, None])
    target_onehot = target[:, :, None] == jnp.arange(devices_all, dtype=jnp.int32)[None, None, :]
    target_hits = jnp.sum(target_onehot.astype(jnp.bfloat16), axis=1)
    counts = jnp.dot(
        ahead_mask.astype(jnp.bfloat16), target_hits, preferred_element_type=jnp.float32
    )
    position = jnp.sum(
        jnp.where(target_onehot, counts[:, None, :], 0.0), axis=2
    ).astype(jnp.int32)
    granted = jnp.sum(
        jnp.where(target_onehot, capacity.reshape(-1)[None, None, :], 0), axis=2
    )
    accepted = position < granted
    in_plane = (copy_choice * lanes + slot % lanes) * cap_size + position
    code = jnp.where(accepted, (slot // lanes) * plane_slots + in_plane, planes * plane_slots)
    weights_kept = jnp.where(accepted, route_weight, jnp.float32(0.0))
    code_hi = (code // 128).astype(jnp.bfloat16)
    code_lo = (code % 128).astype(jnp.bfloat16)
    w_first = lax.reduce_precision(weights_kept, exponent_bits=8, mantissa_bits=7)
    w_rest = weights_kept - w_first
    w_second = lax.reduce_precision(w_rest, exponent_bits=8, mantissa_bits=7)
    w_third = w_rest - w_second
    meta = jnp.concatenate(
        [code_hi, code_lo]
        + [part.astype(jnp.bfloat16) for part in (w_first, w_second, w_third)],
        axis=1,
    )
    meta_size = rows_here * meta.shape[1]
    meta_rows = -(-meta_size // (8 * features)) * 8
    meta_block = jnp.pad(meta.reshape(-1), (0, meta_rows * features - meta_size))
    packed = jnp.concatenate([normed, meta_block.reshape(meta_rows, features)], axis=0)
    gate_up_local = slot_gate_up[0]
    down_local = slot_down[0]
    hidden_units = down_local.shape[0]
    slot_ids = jnp.arange(plane_slots, dtype=jnp.int32)

    def expert(rows_in):
        gate_up = jnp.dot(rows_in, gate_up_local, preferred_element_type=jnp.float32)
        expert_hidden = (
            jax.nn.silu(gate_up[:, :hidden_units]) * gate_up[:, hidden_units:]
        ).astype(jnp.bfloat16)
        return jnp.dot(expert_hidden, down_local, preferred_element_type=jnp.float32).astype(
            jnp.bfloat16
        )

    received = [packed] + [
        lax.ppermute(packed, "eh", [(i, (i + shift) % planes) for i in range(planes)])
        for shift in range(1, planes)
    ]
    hits = []
    weights_in = []
    buffers = []
    for shift, block in enumerate(received):
        meta_s = (
            block[rows_here:]
            .reshape(-1)[:meta_size]
            .reshape(rows_here, meta.shape[1])
            .astype(jnp.float32)
        )
        code_s = meta_s[:, :picks_row] * 128 + meta_s[:, picks_row : 2 * picks_row]
        local = code_s.astype(jnp.int32) - my_plane * plane_slots
        weights_in.append(
            (meta_s[:, 2 * picks_row : 3 * picks_row] + meta_s[:, 3 * picks_row : 4 * picks_row])
            + meta_s[:, 4 * picks_row :]
        )
        hit = local[None, :, :] == slot_ids[:, None, None]
        hits.append(hit)
        dispatch = jnp.any(hit, axis=2).astype(jnp.bfloat16)
        buffer = jnp.dot(dispatch, block[:rows_here], preferred_element_type=jnp.float32)
        buffers.append(buffer.astype(jnp.bfloat16).reshape(groups * lanes, cap_size, features))
    arrived = lax.all_to_all(
        jnp.stack(buffers, axis=1), PLANE_AXES, split_axis=0, concat_axis=0, tiled=True
    )
    produced = expert(arrived.reshape(-1, features)).reshape(arrived.shape)
    partials = [None] * planes
    for shift in list(range(1, planes)) + [0]:
        returned = lax.all_to_all(
            produced[:, shift], PLANE_AXES, split_axis=0, concat_axis=0, tiled=True
        )
        combine = jnp.sum(jnp.where(hits[shift], weights_in[shift][None, :, :], 0.0), axis=2)
        partial = jnp.dot(
            combine.T,
            returned.reshape(plane_slots, features).astype(jnp.float32),
            precision=lax.Precision.HIGHEST,
            preferred_element_type=jnp.float32,
        )
        if shift:
            back = [((i + shift) % planes, i) for i in range(planes)]
            partial = lax.ppermute(partial.astype(jnp.bfloat16), "eh", back).astype(jnp.float32)
        partials[shift] = partial
    mixture = partials[0]
    for partial in partials[1:]:
        mixture = mixture + partial
    return rms_scale(hidden_state.astype(jnp.float32) + mixture, post_gain).astype(jnp.bfloat16)


def plane_split(devices):
    row = devices[0]
    try:
        coords = [tuple(d.coords) for d in row]
    except AttributeError:
        return 1, len(row)
    best = 0
    for axis in range(len(coords[0])):
        changes = [e for e in range(len(row)) if coords[e][axis] != coords[0][axis]]
        if changes:
            best = max(best, changes[0])
    if best == 0 or len(row) % best or (len(row) // best) % 2:
        return 1, len(row)
    return 2, len(row) // 2


def solution(mesh):
    devices = np.asarray(mesh.devices)
    planes, lanes = plane_split(devices)
    fine = Mesh(devices.reshape(devices.shape[0], planes, lanes), ROWS_AXES)
    rows = P(ROWS_AXES, None)
    placed = (
        rows,
        rows,
        P(None, "grp"),
        P(),
        P(),
        P(SLOT_AXES, None, None),
        P(SLOT_AXES, None, None),
        rows,
        rows,
        P(),
        P(ROWS_AXES),
        P(ROWS_AXES),
        P(),
        rows,
    )
    return jax.shard_map(on_device, mesh=fine, in_specs=placed, out_specs=rows, check_vma=False)
```

```python
import jax
import jax.numpy as jnp
import numpy as np
from jax import lax
from jax.sharding import Mesh
from jax.sharding import PartitionSpec as P

ROWS_AXES = ("grp", "eh", "el")
SLOT_AXES = ("eh", "el")
PLANE_AXES = ("grp", "el")


def rms_scale(values, gain):
    meansq = jnp.mean(values * values, axis=-1, keepdims=True)
    return values * lax.rsqrt(meansq + 1e-06) * gain


def on_device(
    attention,
    residual,
    out_proj,
    pre_gain,
    post_gain,
    slot_gate_up,
    slot_down,
    expert_ids,
    copy_choice,
    placement,
    request_age,
    decode_flag,
    capacity,
    route_weight,
):
    groups = lax.axis_size("grp")
    planes = lax.axis_size("eh")
    lanes = lax.axis_size("el")
    owners = planes * lanes
    devices_all = groups * owners
    rows_here = attention.shape[0]
    features = attention.shape[1]
    picks_row = expert_ids.shape[1]
    cap_size = max(2, rows_here * picks_row // devices_all)
    plane_slots = groups * lanes * cap_size
    my_plane = lax.axis_index("eh")

    me_grp = lax.axis_index("grp")
    blocks = [None] * groups
    blocks[0] = jnp.dot(attention, out_proj, preferred_element_type=jnp.float32)
    for shift in range(1, groups):
        ahead = [(g, (g + shift) % groups) for g in range(groups)]
        back = [(b, a) for a, b in ahead]
        visiting = lax.ppermute(attention, "grp", ahead)
        done = jnp.dot(visiting, out_proj, preferred_element_type=jnp.float32)
        blocks[shift] = lax.ppermute(done, "grp", back)
    stacked = jnp.stack(blocks, axis=0)
    order_cols = (jnp.arange(groups, dtype=jnp.int32) - me_grp) % groups
    attn_proj = jnp.concatenate(
        [jnp.take(stacked, order_cols[j], axis=0) for j in range(groups)], axis=1
    )
    hidden_state = (residual.astype(jnp.float32) + attn_proj).astype(jnp.bfloat16)
    normed = rms_scale(hidden_state.astype(jnp.float32), pre_gain).astype(jnp.bfloat16)

    experts_all = placement.shape[0]
    slot_table = jnp.arange(owners, dtype=jnp.int32)
    matches = (placement[None, :] == jnp.arange(experts_all, dtype=jnp.int32)[:, None]).astype(
        jnp.int32
    )
    slot_of = jnp.sum(slot_table[None, :] * matches, axis=1)
    expert_hits = (
        expert_ids[:, :, None] == jnp.arange(experts_all, dtype=jnp.int32)[None, None, :]
    ).astype(jnp.int32)
    slot = jnp.sum(expert_hits * slot_of[None, None, :], axis=2)
    target = copy_choice * owners + slot
    priority = decode_flag * 1048576 + request_age
    order = jnp.arange(rows_here, dtype=jnp.int32)
    ahead_mask = (priority[None, :] > priority[:, None]) | (
        priority[None, :] == priority[:, None]
    ) & (order[None, :] < order[:, None])
    target_onehot = target[:, :, None] == jnp.arange(devices_all, dtype=jnp.int32)[None, None, :]
    target_hits = jnp.sum(target_onehot.astype(jnp.bfloat16), axis=1)
    counts = jnp.dot(
        ahead_mask.astype(jnp.bfloat16), target_hits, preferred_element_type=jnp.float32
    )
    position = jnp.sum(
        jnp.where(target_onehot, counts[:, None, :], 0.0), axis=2
    ).astype(jnp.int32)
    granted = jnp.sum(
        jnp.where(target_onehot, capacity.reshape(-1)[None, None, :], 0), axis=2
    )
    accepted = position < granted
    in_plane = (copy_choice * lanes + slot % lanes) * cap_size + position
    code = jnp.where(accepted, (slot // lanes) * plane_slots + in_plane, planes * plane_slots)
    weights_kept = jnp.where(accepted, route_weight, jnp.float32(0.0))
    code_hi = (code // 128).astype(jnp.bfloat16)
    code_lo = (code % 128).astype(jnp.bfloat16)
    w_first = lax.reduce_precision(weights_kept, exponent_bits=8, mantissa_bits=7)
    w_rest = weights_kept - w_first
    w_second = lax.reduce_precision(w_rest, exponent_bits=8, mantissa_bits=7)
    w_third = w_rest - w_second
    meta = jnp.concatenate(
        [code_hi, code_lo]
        + [part.astype(jnp.bfloat16) for part in (w_first, w_second, w_third)],
        axis=1,
    )
    meta_size = rows_here * meta.shape[1]
    meta_rows = -(-meta_size // (8 * features)) * 8
    meta_block = jnp.pad(meta.reshape(-1), (0, meta_rows * features - meta_size))
    packed = jnp.concatenate([normed, meta_block.reshape(meta_rows, features)], axis=0)
    gate_up_local = slot_gate_up[0]
    down_local = slot_down[0]
    hidden_units = down_local.shape[0]
    slot_ids = jnp.arange(plane_slots, dtype=jnp.int32)

    def expert(rows_in):
        gate_up = jnp.dot(rows_in, gate_up_local, preferred_element_type=jnp.float32)
        expert_hidden = (
            jax.nn.silu(gate_up[:, :hidden_units]) * gate_up[:, hidden_units:]
        ).astype(jnp.bfloat16)
        return jnp.dot(expert_hidden, down_local, preferred_element_type=jnp.float32).astype(
            jnp.bfloat16
        )

    received = [packed] + [
        lax.ppermute(packed, "eh", [(i, (i + shift) % planes) for i in range(planes)])
        for shift in range(1, planes)
    ]
    hits = []
    weights_in = []
    buffers = []
    for shift, block in enumerate(received):
        meta_s = (
            block[rows_here:]
            .reshape(-1)[:meta_size]
            .reshape(rows_here, meta.shape[1])
            .astype(jnp.float32)
        )
        code_s = meta_s[:, :picks_row] * 128 + meta_s[:, picks_row : 2 * picks_row]
        local = code_s.astype(jnp.int32) - my_plane * plane_slots
        weights_in.append(
            (meta_s[:, 2 * picks_row : 3 * picks_row] + meta_s[:, 3 * picks_row : 4 * picks_row])
            + meta_s[:, 4 * picks_row :]
        )
        hit = local[None, :, :] == slot_ids[:, None, None]
        hits.append(hit)
        dispatch = jnp.any(hit, axis=2).astype(jnp.bfloat16)
        buffer = jnp.dot(dispatch, block[:rows_here], preferred_element_type=jnp.float32)
        buffers.append(buffer.astype(jnp.bfloat16).reshape(groups * lanes, cap_size, features))
    arrived = lax.all_to_all(
        jnp.stack(buffers, axis=0), PLANE_AXES, split_axis=1, concat_axis=1, tiled=True
    )
    partials = [None] * planes
    for shift in list(range(1, planes)) + [0]:
        produced = expert(arrived[shift].reshape(-1, features)).reshape(arrived.shape[1:])
        returned = lax.all_to_all(produced, PLANE_AXES, split_axis=0, concat_axis=0, tiled=True)
        combine = jnp.sum(jnp.where(hits[shift], weights_in[shift][None, :, :], 0.0), axis=2)
        partial = jnp.dot(
            combine.T,
            returned.reshape(plane_slots, features).astype(jnp.float32),
            precision=lax.Precision.HIGHEST,
            preferred_element_type=jnp.float32,
        )
        if shift:
            back = [((i + shift) % planes, i) for i in range(planes)]
            partial = lax.ppermute(partial.astype(jnp.bfloat16), "eh", back).astype(jnp.float32)
        partials[shift] = partial
    mixture = partials[0]
    for partial in partials[1:]:
        mixture = mixture + partial
    return rms_scale(hidden_state.astype(jnp.float32) + mixture, post_gain).astype(jnp.bfloat16)


def plane_split(devices):
    row = devices[0]
    try:
        coords = [tuple(d.coords) for d in row]
    except AttributeError:
        return 1, len(row)
    best = 0
    for axis in range(len(coords[0])):
        changes = [e for e in range(len(row)) if coords[e][axis] != coords[0][axis]]
        if changes:
            best = max(best, changes[0])
    if best == 0 or len(row) % best or (len(row) // best) % 2:
        return 1, len(row)
    return 2, len(row) // 2


def solution(mesh):
    devices = np.asarray(mesh.devices)
    planes, lanes = plane_split(devices)
    fine = Mesh(devices.reshape(devices.shape[0], planes, lanes), ROWS_AXES)
    rows = P(ROWS_AXES, None)
    placed = (
        rows,
        rows,
        P(None, "grp"),
        P(),
        P(),
        P(SLOT_AXES, None, None),
        P(SLOT_AXES, None, None),
        rows,
        rows,
        P(),
        P(ROWS_AXES),
        P(ROWS_AXES),
        P(),
        rows,
    )
    return jax.shard_map(on_device, mesh=fine, in_specs=placed, out_specs=rows, check_vma=False)
```

```python
import jax
import jax.numpy as jnp
import numpy as np
from jax import lax
from jax.sharding import Mesh
from jax.sharding import PartitionSpec as P

ROWS_AXES = ("grp", "eh", "el")
SLOT_AXES = ("eh", "el")
PLANE_AXES = ("grp", "el")


def rms_scale(values, gain):
    meansq = jnp.mean(values * values, axis=-1, keepdims=True)
    return values * lax.rsqrt(meansq + 1e-06) * gain


def on_device(
    attention,
    residual,
    out_proj,
    pre_gain,
    post_gain,
    slot_gate_up,
    slot_down,
    expert_ids,
    copy_choice,
    placement,
    request_age,
    decode_flag,
    capacity,
    route_weight,
):
    groups = lax.axis_size("grp")
    planes = lax.axis_size("eh")
    lanes = lax.axis_size("el")
    owners = planes * lanes
    devices_all = groups * owners
    rows_here = attention.shape[0]
    features = attention.shape[1]
    picks_row = expert_ids.shape[1]
    cap_size = max(2, rows_here * picks_row // devices_all)
    plane_slots = groups * lanes * cap_size
    my_plane = lax.axis_index("eh")

    me_grp = lax.axis_index("grp")
    blocks = [None] * groups
    blocks[0] = jnp.dot(attention, out_proj, preferred_element_type=jnp.float32)
    for shift in range(1, groups):
        ahead = [(g, (g + shift) % groups) for g in range(groups)]
        back = [(b, a) for a, b in ahead]
        half = rows_here // 2
        pieces = []
        for lo in (0, half):
            visiting = lax.ppermute(attention[lo : lo + half], "grp", ahead)
            done = jnp.dot(visiting, out_proj, preferred_element_type=jnp.float32)
            pieces.append(lax.ppermute(done, "grp", back))
        blocks[shift] = jnp.concatenate(pieces, axis=0)
    stacked = jnp.stack(blocks, axis=0)
    order_cols = (jnp.arange(groups, dtype=jnp.int32) - me_grp) % groups
    attn_proj = jnp.concatenate(
        [jnp.take(stacked, order_cols[j], axis=0) for j in range(groups)], axis=1
    )
    hidden_state = (residual.astype(jnp.float32) + attn_proj).astype(jnp.bfloat16)
    normed = rms_scale(hidden_state.astype(jnp.float32), pre_gain).astype(jnp.bfloat16)

    experts_all = placement.shape[0]
    slot_table = jnp.arange(owners, dtype=jnp.int32)
    matches = (placement[None, :] == jnp.arange(experts_all, dtype=jnp.int32)[:, None]).astype(
        jnp.int32
    )
    slot_of = jnp.sum(slot_table[None, :] * matches, axis=1)
    expert_hits = (
        expert_ids[:, :, None] == jnp.arange(experts_all, dtype=jnp.int32)[None, None, :]
    ).astype(jnp.int32)
    slot = jnp.sum(expert_hits * slot_of[None, None, :], axis=2)
    target = copy_choice * owners + slot
    priority = decode_flag * 1048576 + request_age
    order = jnp.arange(rows_here, dtype=jnp.int32)
    ahead_mask = (priority[None, :] > priority[:, None]) | (
        priority[None, :] == priority[:, None]
    ) & (order[None, :] < order[:, None])
    target_onehot = target[:, :, None] == jnp.arange(devices_all, dtype=jnp.int32)[None, None, :]
    target_hits = jnp.sum(target_onehot.astype(jnp.bfloat16), axis=1)
    counts = jnp.dot(
        ahead_mask.astype(jnp.bfloat16), target_hits, preferred_element_type=jnp.float32
    )
    position = jnp.sum(
        jnp.where(target_onehot, counts[:, None, :], 0.0), axis=2
    ).astype(jnp.int32)
    granted = jnp.sum(
        jnp.where(target_onehot, capacity.reshape(-1)[None, None, :], 0), axis=2
    )
    accepted = position < granted
    in_plane = (copy_choice * lanes + slot % lanes) * cap_size + position
    code = jnp.where(accepted, (slot // lanes) * plane_slots + in_plane, planes * plane_slots)
    weights_kept = jnp.where(accepted, route_weight, jnp.float32(0.0))
    code_hi = (code // 128).astype(jnp.bfloat16)
    code_lo = (code % 128).astype(jnp.bfloat16)
    w_first = lax.reduce_precision(weights_kept, exponent_bits=8, mantissa_bits=7)
    w_rest = weights_kept - w_first
    w_second = lax.reduce_precision(w_rest, exponent_bits=8, mantissa_bits=7)
    w_third = w_rest - w_second
    meta = jnp.concatenate(
        [code_hi, code_lo]
        + [part.astype(jnp.bfloat16) for part in (w_first, w_second, w_third)],
        axis=1,
    )
    meta_size = rows_here * meta.shape[1]
    meta_rows = -(-meta_size // (8 * features)) * 8
    meta_block = jnp.pad(meta.reshape(-1), (0, meta_rows * features - meta_size))
    packed = jnp.concatenate([normed, meta_block.reshape(meta_rows, features)], axis=0)
    gate_up_local = slot_gate_up[0]
    down_local = slot_down[0]
    hidden_units = down_local.shape[0]
    slot_ids = jnp.arange(plane_slots, dtype=jnp.int32)

    def expert(rows_in):
        gate_up = jnp.dot(rows_in, gate_up_local, preferred_element_type=jnp.float32)
        expert_hidden = (
            jax.nn.silu(gate_up[:, :hidden_units]) * gate_up[:, hidden_units:]
        ).astype(jnp.bfloat16)
        return jnp.dot(expert_hidden, down_local, preferred_element_type=jnp.float32).astype(
            jnp.bfloat16
        )

    received = [packed] + [
        lax.ppermute(packed, "eh", [(i, (i + shift) % planes) for i in range(planes)])
        for shift in range(1, planes)
    ]
    hits = []
    weights_in = []
    buffers = []
    for shift, block in enumerate(received):
        meta_s = (
            block[rows_here:]
            .reshape(-1)[:meta_size]
            .reshape(rows_here, meta.shape[1])
            .astype(jnp.float32)
        )
        code_s = meta_s[:, :picks_row] * 128 + meta_s[:, picks_row : 2 * picks_row]
        local = code_s.astype(jnp.int32) - my_plane * plane_slots
        weights_in.append(
            (meta_s[:, 2 * picks_row : 3 * picks_row] + meta_s[:, 3 * picks_row : 4 * picks_row])
            + meta_s[:, 4 * picks_row :]
        )
        hit = local[None, :, :] == slot_ids[:, None, None]
        hits.append(hit)
        dispatch = jnp.any(hit, axis=2).astype(jnp.bfloat16)
        buffer = jnp.dot(dispatch, block[:rows_here], preferred_element_type=jnp.float32)
        buffers.append(buffer.astype(jnp.bfloat16).reshape(groups * lanes, cap_size, features))
    arrived = lax.all_to_all(
        jnp.stack(buffers, axis=1), PLANE_AXES, split_axis=0, concat_axis=0, tiled=True
    )
    produced = expert(arrived.reshape(-1, features)).reshape(arrived.shape)
    partials = [None] * planes
    for shift in list(range(1, planes)) + [0]:
        returned = lax.all_to_all(
            produced[:, shift], PLANE_AXES, split_axis=0, concat_axis=0, tiled=True
        )
        combine = jnp.sum(jnp.where(hits[shift], weights_in[shift][None, :, :], 0.0), axis=2)
        partial = jnp.dot(
            combine.T,
            returned.reshape(plane_slots, features).astype(jnp.float32),
            precision=lax.Precision.HIGHEST,
            preferred_element_type=jnp.float32,
        )
        if shift:
            back = [((i + shift) % planes, i) for i in range(planes)]
            partial = lax.ppermute(partial.astype(jnp.bfloat16), "eh", back).astype(jnp.float32)
        partials[shift] = partial
    mixture = partials[0]
    for partial in partials[1:]:
        mixture = mixture + partial
    return rms_scale(hidden_state.astype(jnp.float32) + mixture, post_gain).astype(jnp.bfloat16)


def plane_split(devices):
    row = devices[0]
    try:
        coords = [tuple(d.coords) for d in row]
    except AttributeError:
        return 1, len(row)
    best = 0
    for axis in range(len(coords[0])):
        changes = [e for e in range(len(row)) if coords[e][axis] != coords[0][axis]]
        if changes:
            best = max(best, changes[0])
    if best == 0 or len(row) % best or (len(row) // best) % 2:
        return 1, len(row)
    return 2, len(row) // 2


def solution(mesh):
    devices = np.asarray(mesh.devices)
    planes, lanes = plane_split(devices)
    fine = Mesh(devices.reshape(devices.shape[0], planes, lanes), ROWS_AXES)
    rows = P(ROWS_AXES, None)
    placed = (
        rows,
        rows,
        P(None, "grp"),
        P(),
        P(),
        P(SLOT_AXES, None, None),
        P(SLOT_AXES, None, None),
        rows,
        rows,
        P(),
        P(ROWS_AXES),
        P(ROWS_AXES),
        P(),
        rows,
    )
    return jax.shard_map(on_device, mesh=fine, in_specs=placed, out_specs=rows, check_vma=False)
```

```python
import jax
import jax.numpy as jnp
import numpy as np
from jax import lax
from jax.sharding import Mesh
from jax.sharding import PartitionSpec as P

ROWS_AXES = ("grp", "eh", "el")
SLOT_AXES = ("eh", "el")
PLANE_AXES = ("grp", "el")


def rms_scale(values, gain):
    meansq = jnp.mean(values * values, axis=-1, keepdims=True)
    return values * lax.rsqrt(meansq + 1e-06) * gain


def on_device(
    attention,
    residual,
    out_proj,
    pre_gain,
    post_gain,
    slot_gate_up,
    slot_down,
    expert_ids,
    copy_choice,
    placement,
    request_age,
    decode_flag,
    capacity,
    route_weight,
):
    groups = lax.axis_size("grp")
    planes = lax.axis_size("eh")
    lanes = lax.axis_size("el")
    owners = planes * lanes
    devices_all = groups * owners
    rows_here = attention.shape[0]
    features = attention.shape[1]
    picks_row = expert_ids.shape[1]
    cap_size = max(2, rows_here * picks_row // devices_all)
    plane_slots = groups * lanes * cap_size
    my_plane = lax.axis_index("eh")

    me_grp = lax.axis_index("grp")
    blocks = [None] * groups
    blocks[0] = jnp.dot(attention, out_proj, preferred_element_type=jnp.float32)
    for shift in range(1, groups):
        ahead = [(g, (g + shift) % groups) for g in range(groups)]
        back = [(b, a) for a, b in ahead]
        visiting = lax.ppermute(attention, "grp", ahead)
        done = jnp.dot(visiting, out_proj, preferred_element_type=jnp.float32)
        blocks[shift] = lax.ppermute(done, "grp", back)
    stacked = jnp.stack(blocks, axis=0)
    order_cols = (jnp.arange(groups, dtype=jnp.int32) - me_grp) % groups
    attn_proj = jnp.concatenate(
        [jnp.take(stacked, order_cols[j], axis=0) for j in range(groups)], axis=1
    )
    hidden_state = (residual.astype(jnp.float32) + attn_proj).astype(jnp.bfloat16)
    normed = rms_scale(hidden_state.astype(jnp.float32), pre_gain).astype(jnp.bfloat16)

    experts_all = placement.shape[0]
    slot_table = jnp.arange(owners, dtype=jnp.int32)
    matches = (placement[None, :] == jnp.arange(experts_all, dtype=jnp.int32)[:, None]).astype(
        jnp.int32
    )
    slot_of = jnp.sum(slot_table[None, :] * matches, axis=1)
    expert_hits = (
        expert_ids[:, :, None] == jnp.arange(experts_all, dtype=jnp.int32)[None, None, :]
    ).astype(jnp.int32)
    slot = jnp.sum(expert_hits * slot_of[None, None, :], axis=2)
    target = copy_choice * owners + slot
    priority = decode_flag * 1048576 + request_age
    order = jnp.arange(rows_here, dtype=jnp.int32)
    ahead_mask = (priority[None, :] > priority[:, None]) | (
        priority[None, :] == priority[:, None]
    ) & (order[None, :] < order[:, None])
    target_onehot = target[:, :, None] == jnp.arange(devices_all, dtype=jnp.int32)[None, None, :]
    target_hits = jnp.sum(target_onehot.astype(jnp.bfloat16), axis=1)
    counts = jnp.dot(
        ahead_mask.astype(jnp.bfloat16), target_hits, preferred_element_type=jnp.float32
    )
    position = jnp.sum(
        jnp.where(target_onehot, counts[:, None, :], 0.0), axis=2
    ).astype(jnp.int32)
    granted = jnp.sum(
        jnp.where(target_onehot, capacity.reshape(-1)[None, None, :], 0), axis=2
    )
    accepted = position < granted
    in_plane = (copy_choice * lanes + slot % lanes) * cap_size + position
    code = jnp.where(accepted, (slot // lanes) * plane_slots + in_plane, planes * plane_slots)
    weights_kept = jnp.where(accepted, route_weight, jnp.float32(0.0))
    code_hi = (code // 128).astype(jnp.bfloat16)
    code_lo = (code % 128).astype(jnp.bfloat16)
    w_first = lax.reduce_precision(weights_kept, exponent_bits=8, mantissa_bits=7)
    w_rest = weights_kept - w_first
    w_second = lax.reduce_precision(w_rest, exponent_bits=8, mantissa_bits=7)
    w_third = w_rest - w_second
    meta = jnp.concatenate(
        [code_hi, code_lo]
        + [part.astype(jnp.bfloat16) for part in (w_first, w_second, w_third)],
        axis=1,
    )
    meta_size = rows_here * meta.shape[1]
    meta_rows = -(-meta_size // (8 * features)) * 8
    meta_block = jnp.pad(meta.reshape(-1), (0, meta_rows * features - meta_size))
    packed = jnp.concatenate([normed, meta_block.reshape(meta_rows, features)], axis=0)
    gate_up_local = slot_gate_up[0]
    down_local = slot_down[0]
    hidden_units = down_local.shape[0]
    slot_ids = jnp.arange(plane_slots, dtype=jnp.int32)

    def expert(rows_in):
        gate_up = jnp.dot(rows_in, gate_up_local, preferred_element_type=jnp.float32)
        expert_hidden = (
            jax.nn.silu(gate_up[:, :hidden_units]) * gate_up[:, hidden_units:]
        ).astype(jnp.bfloat16)
        return jnp.dot(expert_hidden, down_local, preferred_element_type=jnp.float32).astype(
            jnp.bfloat16
        )

    received = [packed] + [
        lax.ppermute(packed, "eh", [(i, (i + shift) % planes) for i in range(planes)])
        for shift in range(1, planes)
    ]
    hits = []
    weights_in = []
    buffers = []
    for shift, block in enumerate(received):
        meta_s = (
            block[rows_here:]
            .reshape(-1)[:meta_size]
            .reshape(rows_here, meta.shape[1])
            .astype(jnp.float32)
        )
        code_s = meta_s[:, :picks_row] * 128 + meta_s[:, picks_row : 2 * picks_row]
        local = code_s.astype(jnp.int32) - my_plane * plane_slots
        weights_in.append(
            (meta_s[:, 2 * picks_row : 3 * picks_row] + meta_s[:, 3 * picks_row : 4 * picks_row])
            + meta_s[:, 4 * picks_row :]
        )
        if shift == 0:
            local = code - my_plane * plane_slots
            weights_in[0] = weights_kept
        hit = local[None, :, :] == slot_ids[:, None, None]
        hits.append(hit)
        dispatch = jnp.any(hit, axis=2).astype(jnp.bfloat16)
        buffer = jnp.dot(dispatch, block[:rows_here], preferred_element_type=jnp.float32)
        buffers.append(buffer.astype(jnp.bfloat16).reshape(groups * lanes, cap_size, features))
    arrived = lax.all_to_all(
        jnp.stack(buffers, axis=1), PLANE_AXES, split_axis=0, concat_axis=0, tiled=True
    )
    produced = expert(arrived.reshape(-1, features)).reshape(arrived.shape)
    partials = [None] * planes
    for shift in list(range(1, planes)) + [0]:
        returned = lax.all_to_all(
            produced[:, shift], PLANE_AXES, split_axis=0, concat_axis=0, tiled=True
        )
        combine = jnp.sum(jnp.where(hits[shift], weights_in[shift][None, :, :], 0.0), axis=2)
        partial = jnp.dot(
            combine.T,
            returned.reshape(plane_slots, features).astype(jnp.float32),
            precision=lax.Precision.HIGHEST,
            preferred_element_type=jnp.float32,
        )
        if shift:
            back = [((i + shift) % planes, i) for i in range(planes)]
            partial = lax.ppermute(partial.astype(jnp.bfloat16), "eh", back).astype(jnp.float32)
        partials[shift] = partial
    mixture = partials[0]
    for partial in partials[1:]:
        mixture = mixture + partial
    return rms_scale(hidden_state.astype(jnp.float32) + mixture, post_gain).astype(jnp.bfloat16)


def plane_split(devices):
    row = devices[0]
    try:
        coords = [tuple(d.coords) for d in row]
    except AttributeError:
        return 1, len(row)
    best = 0
    for axis in range(len(coords[0])):
        changes = [e for e in range(len(row)) if coords[e][axis] != coords[0][axis]]
        if changes:
            best = max(best, changes[0])
    if best == 0 or len(row) % best or (len(row) // best) % 2:
        return 1, len(row)
    return 2, len(row) // 2


def solution(mesh):
    devices = np.asarray(mesh.devices)
    planes, lanes = plane_split(devices)
    fine = Mesh(devices.reshape(devices.shape[0], planes, lanes), ROWS_AXES)
    rows = P(ROWS_AXES, None)
    placed = (
        rows,
        rows,
        P(None, "grp"),
        P(),
        P(),
        P(SLOT_AXES, None, None),
        P(SLOT_AXES, None, None),
        rows,
        rows,
        P(),
        P(ROWS_AXES),
        P(ROWS_AXES),
        P(),
        rows,
    )
    return jax.shard_map(on_device, mesh=fine, in_specs=placed, out_specs=rows, check_vma=False)
```
